128 devices in a mesh: group: 8 (over x, core), local: 16 (over z, y).
Axes of the slice: x: 4, y: 4, z: 4, core: 2. Of those that a mesh axis runs over, the one named last changes fastest.
Arguments:
- tokens: bfloat16 [2048, 4096], P(('group', 'local')), may hold values from -6 to 6
- gate_weight: bfloat16 [128, 4096, 384], P(('group', 'local')), may hold values from -0.09375 to 0.09375
- up_weight: bfloat16 [128, 4096, 384], P(('group', 'local')), may hold values from -0.09375 to 0.09375
- down_weight: bfloat16 [128, 384, 4096], P(('group', 'local')), may hold values from -0.21875 to 0.21875
- out_grad: bfloat16 [2048, 4096], P(('group', 'local')), may hold values from -6 to 6
- group_list: int32 [2048, 4], P(('group', 'local')), may hold values from 0 to 7, all different within a row; in each aligned block of 16 rows (0 to 15, 16 to 31, ...) at most 8 rows name the same one
- expert_pick: int32 [2048, 8], P(('group', 'local')), may hold values from 0 to 31, as said below
- route_weight: bfloat16 [2048, 8], P(('group', 'local')), may hold values from 0.099609375 to 1
Outputs:
- mixed: bfloat16 [2048, 4096], P(('group', 'local'))
- token_grad: bfloat16 [2048, 4096], P(('group', 'local'))
- weight_grad: bfloat16 [2048, 8], P(('group', 'local'))
- gate_grad: bfloat16 [128, 4096, 384], P(('group', 'local'))
- up_grad: bfloat16 [128, 4096, 384], P(('group', 'local'))
- down_grad: bfloat16 [128, 384, 4096], P(('group', 'local'))
The draws below stay inside these ranges and needn't reach their ends.
Inputs may be any that keep to these rules, and one draw needn't show every extreme that they name: `group_list`: each row names 4 different groups; in each aligned block of 16 rows no group is named by more than 8 rows, a bound that some block reaches. `expert_pick`: each row holds 8 different values, exactly 2 of them from j * 8 to (j + 1) * 8 - 1 for each j from 0 to 3.
All inputs are finite; a program needn't handle non-finite values.
Results may differ from the reference program's by a relative error of at most 0.009.
Values may be sent and summed in bfloat16 or wider, within the bound.
No kernel may reach another device: no remote copies, remote signals or barrier semaphores. Data moves between devices by JAX's collectives and lax.ppermute only.
A program may use at most 128 MiB of HBM per device.

```python
import math
import jax
import jax.numpy as jnp
import numpy as np
from jax import lax

D = 4096
HID = 768
HALF = 384
TOPK = 8
GLIM = 4
PER = 2
TOK_DEV = 16
GROUPS = 8
LOCALS = 16
EPG = 8
EXPERTS = 64
TOKENS = 2048
GCAP = 8
CAP2 = 32


def draw_expert_pick(key, part):
    key_order, key_shuffle = jax.random.split(key, 2)
    order_keys = jax.random.split(key_order, TOKENS * GLIM)
    orders = jax.vmap(lambda one_key: jax.random.permutation(one_key, EPG))(order_keys)
    leading = orders[:, :PER].reshape(TOKENS, GLIM, PER)
    picks = (leading + EPG * jnp.arange(GLIM, dtype=jnp.int32)[None, :, None]).reshape(TOKENS, TOPK)
    shuffle_keys = jax.random.split(key_shuffle, TOKENS)
    shuffles = jax.vmap(lambda one_key: jax.random.permutation(one_key, TOPK))(shuffle_keys)
    return jnp.take_along_axis(picks, shuffles, axis=1).astype(jnp.int32)


def block_levels(stream_key, extent, pieces, low, top_value):
    factor_of = 1.0
    for axis_at, shards_of in pieces:
        heights = jax.random.uniform(jax.random.fold_in(jax.random.fold_in(stream_key, 6), axis_at), (shards_of,), jnp.float32, low / len(pieces), top_value / len(pieces))
        factor_of = factor_of * jnp.repeat(jnp.exp(heights), extent[axis_at] // shards_of).reshape((-1,) + (1,) * (len(extent) - 1 - axis_at))
    return factor_of


def shared_out(rng, own, number, rows, count, top, reach, lean):
    sequence = jax.random.permutation(rng, count)
    heavy_load, common = load_shares(count, rows * top, reach, lean, True), load_shares(count, rows * top, reach, lean, False)
    places = jnp.arange(count)

    def named(sizes, rotation):
        used = int((sizes > 0).sum())
        fixed = max(1, used // 4)
        shifted = fixed + (places - fixed + rotation * (used - fixed)) % max(1, count - fixed)
        return jnp.zeros((count,), jnp.int32).at[sequence[jnp.where(places < fixed, places, shifted)]].set(jnp.asarray(sizes, jnp.int32))

    sizes = jnp.where(number % 4 == 0, named(heavy_load, number // 4), named(common, number - number // 4 - 1))
    mixed = jax.random.permutation(jax.random.fold_in(own, 3), count)
    giver, taker = mixed[0:count // 2 * 2:2], mixed[1:count // 2 * 2:2]
    room = jnp.minimum(sizes[giver] - 1, reach - sizes[taker]) // 2
    room = jnp.where((giver == sequence[0]) | (taker == sequence[0]) | (sizes[taker] == 0), 0, jnp.maximum(room, 0))
    shifted = jax.random.randint(jax.random.fold_in(own, 4), (count // 2,), 0, 1 << 20) % (room + 1)
    sizes = sizes.at[giver].add(-shifted).at[taker].add(shifted)
    items = jnp.searchsorted(jnp.cumsum(sizes), jnp.arange(rows * top), side="right").astype(jnp.int32)
    grid = items.reshape(top, rows).T
    grid = grid[jax.random.permutation(jax.random.fold_in(own, 1), rows)]
    rotation = jax.random.randint(jax.random.fold_in(own, 2), (rows, 1), 0, top)
    return jnp.take_along_axis(grid, (jnp.arange(top)[None, :] + rotation) % top, axis=1)


def load_shares(amount, total, reach, lean, full):
    portions = [(1 << 20) // math.isqrt(grade ** lean) + 1 for grade in range(1, amount + 1)]
    largest = reach if full else min(reach, max(-(-total // amount), total * portions[0] // sum(portions)))
    least = 1 if total - largest >= amount - 1 else 0
    counts, rest = [largest] + [least] * (amount - 1), total - largest - least * (amount - 1)
    while rest > 0:
        free = [i for i in range(1, amount) if counts[i] < largest] or [i for i in range(1, amount) if counts[i] < reach]
        whole, remaining = sum([portions[i] for i in free]), rest
        for i in free:
            addition = min(reach - counts[i], max(1, remaining * portions[i] // whole), rest)
            counts[i] = counts[i] + addition
            rest = rest - addition
    return np.array(counts)


def centred(key, extent, deviation, most, cuts=(), held_as=jnp.bfloat16):
    values = jax.random.normal(key, extent, jnp.float32) * deviation
    if len(cuts) > 0:
        values = block_levels(key, extent, cuts, -0.22, 0.18) * values
    return jnp.clip(values, min=-most, max=most).astype(held_as)


def setup_inputs(seed: int = 0) -> dict:
    key_list = jax.random.split(jax.random.key(seed), 9)
    tokens = centred(key_list[0], (TOKENS, D), 1.0, 6.0, ((0, 128),))
    gate_weight = centred(key_list[1], (2 * EXPERTS, D, HALF), D ** -0.5, 0.09375, ((0, 128),))
    up_weight = centred(key_list[2], (2 * EXPERTS, D, HALF), D ** -0.5, 0.09375, ((0, 128),))
    down_weight = centred(key_list[3], (2 * EXPERTS, HALF, D), HID ** -0.5, 0.21875, ((0, 128),))
    out_grad = centred(key_list[4], (TOKENS, D), 1.0, 6.0, ((0, 128),))
    group_list_keys = jax.random.split(jax.random.fold_in(key_list[5], 1), TOKENS // TOK_DEV)
    group_list_turns = jax.random.permutation(jax.random.fold_in(key_list[5], 3), TOKENS // TOK_DEV)
    group_list = jax.vmap(lambda own, number: shared_out(jax.random.fold_in(key_list[5], 2), own, number, TOK_DEV, GROUPS, GLIM, GCAP, 2))(group_list_keys, group_list_turns).reshape((TOKENS, GLIM))
    expert_pick = draw_expert_pick(jax.random.fold_in(key_list[8], 71), 0)
    route_weight = jnp.clip(jnp.exp(math.log(1.0) - 2.306499 * jax.random.uniform(key_list[7], (TOKENS, TOPK), jnp.float32) ** block_levels(key_list[7], (TOKENS, TOPK), ((0, 128),), -0.2, 0.2)), 0.099609375, 1.0).astype(jnp.bfloat16)
    return {"tokens": tokens, "gate_weight": gate_weight, "up_weight": up_weight, "down_weight": down_weight, "out_grad": out_grad, "group_list": group_list, "expert_pick": expert_pick, "route_weight": route_weight}


def one_expert(items, padded_x, padded_dy):
    table_row, weight_row, gate_pair, up_pair, down_full = items
    gate_full = jnp.concatenate([gate_pair[0], gate_pair[1]], axis=1)
    up_full = jnp.concatenate([up_pair[0], up_pair[1]], axis=1)
    inputs = padded_x[table_row]
    gate = jnp.dot(inputs, gate_full, preferred_element_type=jnp.float32)
    lifted = jnp.dot(inputs, up_full, preferred_element_type=jnp.float32)
    hidden = (gate * jax.nn.sigmoid(gate) * lifted).astype(jnp.bfloat16)
    out_parts = []
    for half_index in range(2):
        lower = half_index * HALF
        upper = lower + HALF
        piece = jnp.dot(hidden[:, lower:upper], down_full[lower:upper], preferred_element_type=jnp.float32)
        out_parts.append(lax.optimization_barrier(piece.astype(jnp.bfloat16)))
    outputs = (out_parts[0].astype(jnp.float32) + out_parts[1].astype(jnp.float32)).astype(jnp.bfloat16)
    cotangent = padded_dy[table_row]
    scaled = (weight_row[:, None] * cotangent.astype(jnp.float32)).astype(jnp.bfloat16)
    dhidden = jnp.dot(scaled, down_full.T, preferred_element_type=jnp.float32)
    sig = jax.nn.sigmoid(gate)
    dgate = (dhidden * lifted * sig * (1.0 + gate * (1.0 - sig))).astype(jnp.bfloat16)
    dlift = (dhidden * gate * sig).astype(jnp.bfloat16)
    grad_gate = jnp.dot(inputs.T, dgate, preferred_element_type=jnp.float32).astype(jnp.bfloat16)
    grad_up = jnp.dot(inputs.T, dlift, preferred_element_type=jnp.float32).astype(jnp.bfloat16)
    grad_down = jnp.dot(hidden.T, scaled, preferred_element_type=jnp.float32).astype(jnp.bfloat16)
    grad_parts = []
    for half_index in range(2):
        lower = half_index * HALF
        upper = lower + HALF
        piece = (jnp.dot(dgate[:, lower:upper], gate_pair[half_index].T, preferred_element_type=jnp.float32)
                 + jnp.dot(dlift[:, lower:upper], up_pair[half_index].T, preferred_element_type=jnp.float32))
        grad_parts.append(lax.optimization_barrier(piece.astype(jnp.bfloat16)))
    in_grad = (grad_parts[0].astype(jnp.float32) + grad_parts[1].astype(jnp.float32)).astype(jnp.bfloat16)
    slot_dw = jnp.sum(cotangent.astype(jnp.float32) * outputs.astype(jnp.float32), axis=1)
    return outputs, in_grad, slot_dw, grad_gate, grad_up, grad_down


def reference(tokens, gate_weight, up_weight, down_weight, out_grad, group_list, expert_pick, route_weight):
    list_slot = expert_pick // EPG
    member = expert_pick % EPG
    chosen_group = jnp.take_along_axis(group_list, list_slot, axis=1)
    expert = chosen_group * EPG + member
    column = (jnp.arange(TOKENS, dtype=jnp.int32) // TOK_DEV) % LOCALS
    flat_key = (expert * LOCALS + column[:, None]).reshape(-1)
    onehot = (flat_key[:, None] == jnp.arange(EXPERTS * LOCALS, dtype=jnp.int32)[None, :]).astype(jnp.int32)
    rank = jnp.take_along_axis(jnp.cumsum(onehot, axis=0), flat_key[:, None], axis=1)[:, 0] - 1
    kept = rank < CAP2
    slot_rows = LOCALS * CAP2
    flat_expert = expert.reshape(-1)
    slot = jnp.where(kept, jnp.repeat(column, TOPK) * CAP2 + rank, slot_rows).astype(jnp.int32)
    token_index = (jnp.arange(TOKENS * TOPK, dtype=jnp.int32) // TOPK).astype(jnp.int32)
    table = jnp.full((EXPERTS, slot_rows), TOKENS, jnp.int32).at[flat_expert, slot].set(token_index, mode="drop")
    weight_flat = route_weight.reshape(-1).astype(jnp.float32)
    weight_table = jnp.zeros((EXPERTS, slot_rows), jnp.float32).at[flat_expert, slot].set(weight_flat, mode="drop")
    padded_x = jnp.concatenate([tokens, jnp.zeros((1, D), tokens.dtype)], axis=0)
    padded_dy = jnp.concatenate([out_grad, jnp.zeros((1, D), out_grad.dtype)], axis=0)
    gates = gate_weight.reshape(EXPERTS, 2, D, HALF)
    ups = up_weight.reshape(EXPERTS, 2, D, HALF)
    downs = down_weight.reshape(EXPERTS, HID, D)
    results = lax.map(lambda items: one_expert(items, padded_x, padded_dy), (table, weight_table, gates, ups, downs))
    outputs, in_grads, slot_dws, grad_gates, grad_ups, grad_downs = results
    position = jnp.where(kept, flat_expert * slot_rows + slot, 0).astype(jnp.int32)
    kept_col = kept[:, None]
    out_rows = jnp.where(kept_col, outputs.reshape(EXPERTS * slot_rows, D)[position], 0.0).astype(jnp.float32)
    grad_rows = jnp.where(kept_col, in_grads.reshape(EXPERTS * slot_rows, D)[position], 0.0).astype(jnp.float32)
    group_hot = (list_slot[:, :, None] == jnp.arange(GLIM, dtype=jnp.int32)[None, None, :]).astype(jnp.float32)
    weights = route_weight.astype(jnp.float32)
    group_sum = jnp.einsum("tkj,tkd->tjd", group_hot * weights[:, :, None], out_rows.reshape(TOKENS, TOPK, D),
                           precision=lax.Precision.HIGHEST).astype(jnp.bfloat16)
    mixed = jnp.sum(group_sum.astype(jnp.float32), axis=1).astype(jnp.bfloat16)
    group_grad = jnp.einsum("tkj,tkd->tjd", group_hot, grad_rows.reshape(TOKENS, TOPK, D),
                            precision=lax.Precision.HIGHEST).astype(jnp.bfloat16)
    token_grad = jnp.sum(group_grad.astype(jnp.float32), axis=1).astype(jnp.bfloat16)
    weight_grad = jnp.where(kept, slot_dws.reshape(-1)[position], 0.0).reshape(TOKENS, TOPK).astype(jnp.bfloat16)
    gate_grad = grad_gates.reshape(EXPERTS, D, 2, HALF).transpose(0, 2, 1, 3).reshape(2 * EXPERTS, D, HALF)
    up_grad = grad_ups.reshape(EXPERTS, D, 2, HALF).transpose(0, 2, 1, 3).reshape(2 * EXPERTS, D, HALF)
    down_grad = grad_downs.reshape(2 * EXPERTS, HALF, D)
    return mixed, token_grad, weight_grad, gate_grad, up_grad, down_grad
```

```python
import jax
import jax.numpy as jnp
from jax import lax
from jax.sharding import PartitionSpec as P

TOPK = 8
GLIM = 4


def to_owners(buffer):
    experts_here, capacity, width = buffer.shape
    doubled = jnp.repeat(buffer, 2, axis=0)
    arrived = lax.all_to_all(doubled, "local", split_axis=0, concat_axis=0, tiled=True)
    return arrived.reshape(-1, width)


def from_owners(partial_value, experts_here):
    width = partial_value.shape[1]
    rounded = partial_value.astype(jnp.bfloat16).reshape(2 * experts_here, -1, width)
    arrived = lax.all_to_all(rounded, "local", split_axis=0, concat_axis=0, tiled=True)
    paired = arrived.reshape(experts_here, 2, -1, width)
    return (paired[:, 0].astype(jnp.float32) + paired[:, 1].astype(jnp.float32)).astype(
        jnp.bfloat16
    )


def expert_forward(inputs, w_gate, w_up, w_down):
    gate = jnp.dot(inputs, w_gate, preferred_element_type=jnp.float32)
    lifted = jnp.dot(inputs, w_up, preferred_element_type=jnp.float32)
    hidden = (gate * jax.nn.sigmoid(gate) * lifted).astype(jnp.bfloat16)
    partial_value = jnp.dot(hidden, w_down, preferred_element_type=jnp.float32)
    return (gate, lifted, hidden, partial_value)


def expert_backward(inputs, scaled, gate, lifted, hidden, w_gate, w_up, w_down):
    contract_last = (((1,), (1,)), ((), ()))
    contract_first = (((0,), (0,)), ((), ()))
    dhidden = lax.dot_general(scaled, w_down, contract_last, preferred_element_type=jnp.float32)
    grad_down = lax.dot_general(
        hidden, scaled, contract_first, preferred_element_type=jnp.float32
    ).astype(jnp.bfloat16)
    sig = jax.nn.sigmoid(gate)
    dgate = (dhidden * lifted * sig * (1.0 + gate * (1.0 - sig))).astype(jnp.bfloat16)
    dlift = (dhidden * gate * sig).astype(jnp.bfloat16)
    grad_gate = lax.dot_general(
        inputs, dgate, contract_first, preferred_element_type=jnp.float32
    ).astype(jnp.bfloat16)
    grad_up = lax.dot_general(
        inputs, dlift, contract_first, preferred_element_type=jnp.float32
    ).astype(jnp.bfloat16)
    input_part = lax.dot_general(
        dgate, w_gate, contract_last, preferred_element_type=jnp.float32
    ) + lax.dot_general(dlift, w_up, contract_last, preferred_element_type=jnp.float32)
    return (grad_gate, grad_up, grad_down, input_part)


def local(
    tokens, gate_weight, up_weight, down_weight, out_grad, group_list, expert_pick, route_weight
):
    tok_count, width = tokens.shape
    group_count = lax.axis_size("group")
    experts_here = lax.axis_size("local") // 2
    capacity = 16 * tok_count // experts_here
    per_group = TOPK // GLIM
    slots = tok_count // 2
    f32 = jnp.float32

    list_slot = expert_pick // experts_here
    member = expert_pick % experts_here
    pick_group = jnp.take_along_axis(group_list, list_slot, axis=1)
    group_ids = jnp.arange(group_count, dtype=jnp.int32)
    hit_group = (pick_group[:, :, None] == group_ids[None, None, :]).astype(jnp.int32)
    order = jnp.cumsum(hit_group, axis=1) - 1
    ordinal = jnp.sum(order * hit_group, axis=2)
    ord_ids = jnp.arange(per_group, dtype=jnp.int32)
    hit_ord = (ordinal[:, :, None] == ord_ids[None, None, :]).astype(jnp.int32)
    sel_tki = hit_group[:, :, :, None] * hit_ord[:, :, None, :]
    member_list = jnp.sum(sel_tki * member[:, :, None, None], axis=1)
    weight_list = jnp.sum(sel_tki.astype(f32) * route_weight.astype(f32)[:, :, None, None], axis=1)
    listed = jnp.sum((group_list[:, :, None] == group_ids[None, None, :]).astype(jnp.int32), axis=1)
    running = jnp.cumsum(listed, axis=0) - 1
    slot_ids = jnp.arange(slots, dtype=jnp.int32)
    placed = (listed.T[:, None, :] > 0) & (running.T[:, None, :] == slot_ids[None, :, None])
    placed_rows = placed.astype(jnp.bfloat16)
    placed_f = placed.astype(f32)
    occupied = jnp.sum(placed.astype(jnp.int32), axis=2)
    slot_member = jnp.einsum("gjt,tgi->gji", placed_f, member_list.astype(f32)) + (
        experts_here * (1 - occupied)
    ).astype(f32)[:, :, None]
    slot_weight = jnp.einsum("gjt,tgi->gji", placed_f, weight_list, precision=lax.Precision.HIGHEST)
    meta = jnp.concatenate([slot_member, slot_weight], axis=2)
    both = jnp.stack([tokens, out_grad], axis=1)
    sent = jnp.einsum(
        "gjt,tcd->gjcd", placed_rows, both, preferred_element_type=f32
    ).astype(jnp.bfloat16)
    arrived = lax.all_to_all(sent, "group", split_axis=0, concat_axis=0, tiled=True)
    arrived_meta = lax.all_to_all(meta, "group", split_axis=0, concat_axis=0, tiled=True)

    rows = arrived.reshape(-1, 2, width)
    arr_x = rows[:, 0]
    arr_dy = rows[:, 1]
    flat_meta = arrived_meta.reshape(-1, 2 * per_group)
    arr_members = flat_meta[:, :per_group].astype(jnp.int32)
    arr_weights = flat_meta[:, per_group:]
    member_ids = jnp.arange(experts_here, dtype=jnp.int32)
    matching = (arr_members[:, :, None] == member_ids[None, None, :]).astype(jnp.int32)
    flags = jnp.sum(matching, axis=1)
    rank = jnp.cumsum(flags, axis=0) - 1
    kept = (flags > 0) & (rank < capacity)
    cap_ids = jnp.arange(capacity, dtype=jnp.int32)
    sel = kept.T[:, None, :] & (rank.T[:, None, :] == cap_ids[None, :, None])
    sel_b = sel.astype(jnp.bfloat16)
    chooser = sel_b[:, :, :, None] * jnp.transpose(matching, (2, 0, 1))[:, None, :, :].astype(
        jnp.bfloat16
    )
    w_member = jnp.sum(matching.astype(f32) * arr_weights[:, :, None], axis=1)
    w_slot = jnp.einsum("msr,rm->ms", sel.astype(f32), w_member, precision=lax.Precision.HIGHEST)
    buf_x = jnp.einsum("msr,rd->msd", sel_b, arr_x, preferred_element_type=f32).astype(
        jnp.bfloat16
    )
    buf_dy = jnp.einsum("msr,rd->msd", sel_b, arr_dy, preferred_element_type=f32)
    buf_scaled = (w_slot[:, :, None] * buf_dy).astype(jnp.bfloat16)

    w_gate = gate_weight[0]
    w_up = up_weight[0]
    w_down = down_weight[0]
    inputs_here = to_owners(buf_x)
    gate, lifted, hidden, partial_value = expert_forward(inputs_here, w_gate, w_up, w_down)
    outputs = from_owners(partial_value, experts_here)
    grads_here = to_owners(buf_scaled)
    grad_gate, grad_up, grad_down, input_part = expert_backward(
        inputs_here, grads_here, gate, lifted, hidden, w_gate, w_up, w_down
    )
    input_grads = from_owners(input_part, experts_here)

    out_pair = jnp.einsum("msri,msd->rid", chooser, outputs, preferred_element_type=f32)
    in_pair = jnp.einsum("msri,msd->rid", chooser, input_grads, preferred_element_type=f32)
    group_sum = jnp.sum(arr_weights[:, :, None] * out_pair, axis=1).astype(jnp.bfloat16)
    group_grad = jnp.sum(in_pair, axis=1).astype(jnp.bfloat16)
    pair_dw = jnp.sum(arr_dy.astype(f32)[:, None, :] * out_pair, axis=2).astype(jnp.bfloat16)
    back = jnp.stack([group_sum, group_grad], axis=1).reshape(group_count, slots, 2, width)
    came_back = lax.all_to_all(back, "group", split_axis=0, concat_axis=0, tiled=True)
    dw_back = lax.all_to_all(
        pair_dw.reshape(group_count, slots, per_group), "group", split_axis=0, concat_axis=0,
        tiled=True,
    )

    per_token = jnp.einsum("gjt,gjcd->tcd", placed_rows, came_back, preferred_element_type=f32)
    mixed = per_token[:, 0].astype(jnp.bfloat16)
    token_grad = per_token[:, 1].astype(jnp.bfloat16)
    dw_token = jnp.einsum(
        "gjt,gji->tgi", placed_f, dw_back.astype(f32), precision=lax.Precision.HIGHEST
    )
    weight_grad = jnp.sum(sel_tki.astype(f32) * dw_token[:, None, :, :], axis=(2, 3)).astype(
        jnp.bfloat16
    )
    return (mixed, token_grad, weight_grad, grad_gate[None], grad_up[None], grad_down[None])


def solution(mesh):
    return jax.shard_map(
        local,
        mesh=mesh,
        in_specs=(
            P(("group", "local"), None),
            P(("group", "local"), None, None),
            P(("group", "local"), None, None),
            P(("group", "local"), None, None),
            P(("group", "local"), None),
            P(("group", "local"), None),
            P(("group", "local"), None),
            P(("group", "local"), None),
        ),
        out_specs=(
            P(("group", "local"), None),
            P(("group", "local"), None),
            P(("group", "local"), None),
            P(("group", "local"), None, None),
            P(("group", "local"), None, None),
            P(("group", "local"), None, None),
        ),
        check_vma=False,
    )
```

```python
import jax
import jax.numpy as jnp
from jax import lax
from jax.sharding import PartitionSpec as P

TOPK = 8
GLIM = 4


def to_owners(doubled):
    width = doubled.shape[-1]
    arrived = lax.all_to_all(doubled, "local", split_axis=0, concat_axis=0, tiled=True)
    return arrived.reshape(-1, width)


def from_owners(partial_value, experts_here):
    width = partial_value.shape[1]
    rounded = partial_value.astype(jnp.bfloat16).reshape(2 * experts_here, -1, width)
    arrived = lax.all_to_all(rounded, "local", split_axis=0, concat_axis=0, tiled=True)
    paired = arrived.reshape(experts_here, 2, -1, width)
    return (paired[:, 0].astype(jnp.float32) + paired[:, 1].astype(jnp.float32)).astype(
        jnp.bfloat16
    )


def expert_forward(inputs, w_gate, w_up, w_down):
    gate = jnp.dot(inputs, w_gate, preferred_element_type=jnp.float32)
    lifted = jnp.dot(inputs, w_up, preferred_element_type=jnp.float32)
    hidden = (gate * jax.nn.sigmoid(gate) * lifted).astype(jnp.bfloat16)
    partial_value = jnp.dot(hidden, w_down, preferred_element_type=jnp.float32)
    return (gate, lifted, hidden, partial_value)


def expert_backward(inputs, scaled, gate, lifted, hidden, w_gate, w_up, w_down):
    contract_last = (((1,), (1,)), ((), ()))
    contract_first = (((0,), (0,)), ((), ()))
    dhidden = lax.dot_general(scaled, w_down, contract_last, preferred_element_type=jnp.float32)
    grad_down = lax.dot_general(
        hidden, scaled, contract_first, preferred_element_type=jnp.float32
    ).astype(jnp.bfloat16)
    sig = jax.nn.sigmoid(gate)
    dgate = (dhidden * lifted * sig * (1.0 + gate * (1.0 - sig))).astype(jnp.bfloat16)
    dlift = (dhidden * gate * sig).astype(jnp.bfloat16)
    grad_gate = lax.dot_general(
        inputs, dgate, contract_first, preferred_element_type=jnp.float32
    ).astype(jnp.bfloat16)
    grad_up = lax.dot_general(
        inputs, dlift, contract_first, preferred_element_type=jnp.float32
    ).astype(jnp.bfloat16)
    input_part = lax.dot_general(
        dgate, w_gate, contract_last, preferred_element_type=jnp.float32
    ) + lax.dot_general(dlift, w_up, contract_last, preferred_element_type=jnp.float32)
    return (grad_gate, grad_up, grad_down, input_part)


def local(
    tokens, gate_weight, up_weight, down_weight, out_grad, group_list, expert_pick, route_weight
):
    tok_count, width = tokens.shape
    group_count = lax.axis_size("group")
    experts_here = lax.axis_size("local") // 2
    capacity = 16 * tok_count // experts_here
    per_group = TOPK // GLIM
    slots = tok_count // 2
    f32 = jnp.float32

    list_slot = expert_pick // experts_here
    member = expert_pick % experts_here
    pick_group = jnp.take_along_axis(group_list, list_slot, axis=1)
    group_ids = jnp.arange(group_count, dtype=jnp.int32)
    hit_group = (pick_group[:, :, None] == group_ids[None, None, :]).astype(jnp.int32)
    order = jnp.cumsum(hit_group, axis=1) - 1
    ordinal = jnp.sum(order * hit_group, axis=2)
    ord_ids = jnp.arange(per_group, dtype=jnp.int32)
    hit_ord = (ordinal[:, :, None] == ord_ids[None, None, :]).astype(jnp.int32)
    sel_tki = hit_group[:, :, :, None] * hit_ord[:, :, None, :]
    member_list = jnp.sum(sel_tki * member[:, :, None, None], axis=1)
    weight_list = jnp.sum(sel_tki.astype(f32) * route_weight.astype(f32)[:, :, None, None], axis=1)
    listed = jnp.sum((group_list[:, :, None] == group_ids[None, None, :]).astype(jnp.int32), axis=1)
    running = jnp.cumsum(listed, axis=0) - 1
    slot_ids = jnp.arange(slots, dtype=jnp.int32)
    placed = (listed.T[:, None, :] > 0) & (running.T[:, None, :] == slot_ids[None, :, None])
    placed_rows = placed.astype(jnp.bfloat16)
    placed_f = placed.astype(f32)
    occupied = jnp.sum(placed.astype(jnp.int32), axis=2)
    slot_member = jnp.einsum("gjt,tgi->gji", placed_f, member_list.astype(f32)) + (
        experts_here * (1 - occupied)
    ).astype(f32)[:, :, None]
    slot_weight = jnp.einsum("gjt,tgi->gji", placed_f, weight_list, precision=lax.Precision.HIGHEST)
    meta = jnp.concatenate([slot_member, slot_weight], axis=2).astype(jnp.bfloat16)
    both = jnp.stack([tokens, out_grad], axis=1)
    sent = jnp.einsum(
        "gjt,tcd->gjcd", placed_rows, both, preferred_element_type=f32
    ).astype(jnp.bfloat16)
    pad = jnp.zeros((group_count, slots, 128 - 2 * per_group), jnp.bfloat16)
    packed = jnp.concatenate([sent.reshape(group_count, slots, 2 * width), meta, pad], axis=2)
    arrived_all = lax.all_to_all(packed, "group", split_axis=0, concat_axis=0, tiled=True)
    arrived = arrived_all[:, :, : 2 * width].reshape(group_count, slots, 2, width)
    arrived_meta = arrived_all[:, :, 2 * width : 2 * width + 2 * per_group].astype(f32)

    rows = arrived.reshape(-1, 2, width)
    arr_x = rows[:, 0]
    arr_dy = rows[:, 1]
    flat_meta = arrived_meta.reshape(-1, 2 * per_group)
    arr_members = flat_meta[:, :per_group].astype(jnp.int32)
    arr_weights = flat_meta[:, per_group:]
    member_ids = jnp.arange(experts_here, dtype=jnp.int32)
    matching = (arr_members[:, :, None] == member_ids[None, None, :]).astype(jnp.int32)
    flags = jnp.sum(matching, axis=1)
    rank = jnp.cumsum(flags, axis=0) - 1
    kept = (flags > 0) & (rank < capacity)
    cap_ids = jnp.arange(capacity, dtype=jnp.int32)
    sel = kept.T[:, None, :] & (rank.T[:, None, :] == cap_ids[None, :, None])
    sel_b = sel.astype(jnp.bfloat16)
    chooser = sel_b[:, :, :, None] * jnp.transpose(matching, (2, 0, 1))[:, None, :, :].astype(
        jnp.bfloat16
    )
    w_member = jnp.sum(matching.astype(f32) * arr_weights[:, :, None], axis=1)
    w_slot = jnp.einsum("msr,rm->ms", sel.astype(f32), w_member, precision=lax.Precision.HIGHEST)
    sel_2 = jnp.repeat(sel_b, 2, axis=0)
    w_slot_2 = jnp.repeat(w_slot, 2, axis=0)
    buf_x = jnp.einsum("msr,rd->msd", sel_2, arr_x, preferred_element_type=f32).astype(
        jnp.bfloat16
    )
    buf_dy = jnp.einsum("msr,rd->msd", sel_2, arr_dy, preferred_element_type=f32)
    buf_scaled = (w_slot_2[:, :, None] * buf_dy).astype(jnp.bfloat16)

    w_gate = gate_weight[0]
    w_up = up_weight[0]
    w_down = down_weight[0]
    inputs_here = to_owners(buf_x)
    gate, lifted, hidden, partial_value = expert_forward(inputs_here, w_gate, w_up, w_down)
    outputs = from_owners(partial_value, experts_here)
    grads_here = to_owners(buf_scaled)
    grad_gate, grad_up, grad_down, input_part = expert_backward(
        inputs_here, grads_here, gate, lifted, hidden, w_gate, w_up, w_down
    )
    input_grads = from_owners(input_part, experts_here)

    out_pair = jnp.einsum("msri,msd->rid", chooser, outputs, preferred_element_type=f32)
    in_pair = jnp.einsum("msri,msd->rid", chooser, input_grads, preferred_element_type=f32)
    group_sum = jnp.sum(arr_weights[:, :, None] * out_pair, axis=1).astype(jnp.bfloat16)
    group_grad = jnp.sum(in_pair, axis=1).astype(jnp.bfloat16)
    pair_dw = jnp.sum(arr_dy.astype(f32)[:, None, :] * out_pair, axis=2).astype(jnp.bfloat16)
    back = jnp.concatenate(
        [
            group_sum.reshape(group_count, slots, width),
            group_grad.reshape(group_count, slots, width),
            pair_dw.reshape(group_count, slots, per_group),
            jnp.zeros((group_count, slots, 128 - per_group), jnp.bfloat16),
        ],
        axis=2,
    )
    back_all = lax.all_to_all(back, "group", split_axis=0, concat_axis=0, tiled=True)
    came_back = back_all[:, :, : 2 * width].reshape(group_count, slots, 2, width)
    dw_back = back_all[:, :, 2 * width : 2 * width + per_group]

    per_token = jnp.einsum("gjt,gjcd->tcd", placed_rows, came_back, preferred_element_type=f32)
    mixed = per_token[:, 0].astype(jnp.bfloat16)
    token_grad = per_token[:, 1].astype(jnp.bfloat16)
    dw_token = jnp.einsum(
        "gjt,gji->tgi", placed_f, dw_back.astype(f32), precision=lax.Precision.HIGHEST
    )
    weight_grad = jnp.sum(sel_tki.astype(f32) * dw_token[:, None, :, :], axis=(2, 3)).astype(
        jnp.bfloat16
    )
    return (mixed, token_grad, weight_grad, grad_gate[None], grad_up[None], grad_down[None])


def solution(mesh):
    return jax.shard_map(
        local,
        mesh=mesh,
        in_specs=(
            P(("group", "local"), None),
            P(("group", "local"), None, None),
            P(("group", "local"), None, None),
            P(("group", "local"), None, None),
            P(("group", "local"), None),
            P(("group", "local"), None),
            P(("group", "local"), None),
            P(("group", "local"), None),
        ),
        out_specs=(
            P(("group", "local"), None),
            P(("group", "local"), None),
            P(("group", "local"), None),
            P(("group", "local"), None, None),
            P(("group", "local"), None, None),
            P(("group", "local"), None, None),
        ),
        check_vma=False,
    )
```

```python
import jax
import jax.numpy as jnp
from jax import lax
from jax.sharding import PartitionSpec as P

TOPK = 8
GLIM = 4


def to_owners(doubled):
    width = doubled.shape[-1]
    arrived = lax.all_to_all(doubled, "local", split_axis=0, concat_axis=0, tiled=True)
    return arrived.reshape(-1, width)


def from_owners(partial_value, experts_here):
    width = partial_value.shape[1]
    rounded = partial_value.astype(jnp.bfloat16).reshape(2 * experts_here, -1, width)
    arrived = lax.all_to_all(rounded, "local", split_axis=0, concat_axis=0, tiled=True)
    paired = arrived.reshape(experts_here, 2, -1, width)
    return (paired[:, 0].astype(jnp.float32) + paired[:, 1].astype(jnp.float32)).astype(
        jnp.bfloat16
    )


def expert_forward(inputs, w_gate, w_up, w_down):
    gate = jnp.dot(inputs, w_gate, preferred_element_type=jnp.float32)
    lifted = jnp.dot(inputs, w_up, preferred_element_type=jnp.float32)
    hidden = (gate * jax.nn.sigmoid(gate) * lifted).astype(jnp.bfloat16)
    partial_value = jnp.dot(hidden, w_down, preferred_element_type=jnp.float32)
    return (gate, lifted, hidden, partial_value)


def expert_backward(inputs, scaled, gate, lifted, hidden, w_gate, w_up, w_down):
    contract_last = (((1,), (1,)), ((), ()))
    contract_first = (((0,), (0,)), ((), ()))
    dhidden = lax.dot_general(scaled, w_down, contract_last, preferred_element_type=jnp.float32)
    grad_down = lax.dot_general(
        hidden, scaled, contract_first, preferred_element_type=jnp.float32
    ).astype(jnp.bfloat16)
    sig = jax.nn.sigmoid(gate)
    dgate = (dhidden * lifted * sig * (1.0 + gate * (1.0 - sig))).astype(jnp.bfloat16)
    dlift = (dhidden * gate * sig).astype(jnp.bfloat16)
    grad_gate = lax.dot_general(
        inputs, dgate, contract_first, preferred_element_type=jnp.float32
    ).astype(jnp.bfloat16)
    grad_up = lax.dot_general(
        inputs, dlift, contract_first, preferred_element_type=jnp.float32
    ).astype(jnp.bfloat16)
    input_part = lax.dot_general(
        dgate, w_gate, contract_last, preferred_element_type=jnp.float32
    ) + lax.dot_general(dlift, w_up, contract_last, preferred_element_type=jnp.float32)
    return (grad_gate, grad_up, grad_down, input_part)


def local(
    tokens, gate_weight, up_weight, down_weight, out_grad, group_list, expert_pick, route_weight
):
    tok_count, width = tokens.shape
    group_count = lax.axis_size("group")
    experts_here = lax.axis_size("local") // 2
    capacity = 16 * tok_count // experts_here
    per_group = TOPK // GLIM
    slots = tok_count // 2
    f32 = jnp.float32

    list_slot = expert_pick // experts_here
    member = expert_pick % experts_here
    pick_group = jnp.take_along_axis(group_list, list_slot, axis=1)
    group_ids = jnp.arange(group_count, dtype=jnp.int32)
    hit_group = (pick_group[:, :, None] == group_ids[None, None, :]).astype(jnp.int32)
    order = jnp.cumsum(hit_group, axis=1) - 1
    ordinal = jnp.sum(order * hit_group, axis=2)
    ord_ids = jnp.arange(per_group, dtype=jnp.int32)
    hit_ord = (ordinal[:, :, None] == ord_ids[None, None, :]).astype(jnp.int32)
    sel_tki = hit_group[:, :, :, None] * hit_ord[:, :, None, :]
    member_list = jnp.sum(sel_tki * member[:, :, None, None], axis=1)
    weight_list = jnp.sum(sel_tki.astype(f32) * route_weight.astype(f32)[:, :, None, None], axis=1)
    listed = jnp.sum((group_list[:, :, None] == group_ids[None, None, :]).astype(jnp.int32), axis=1)
    running = jnp.cumsum(listed, axis=0) - 1
    slot_ids = jnp.arange(slots, dtype=jnp.int32)
    placed = (listed.T[:, None, :] > 0) & (running.T[:, None, :] == slot_ids[None, :, None])
    placed_rows = placed.astype(jnp.bfloat16)
    placed_f = placed.astype(f32)
    occupied = jnp.sum(placed.astype(jnp.int32), axis=2)
    slot_member = jnp.einsum("gjt,tgi->gji", placed_f, member_list.astype(f32)) + (
        experts_here * (1 - occupied)
    ).astype(f32)[:, :, None]
    slot_weight = jnp.einsum("gjt,tgi->gji", placed_f, weight_list, precision=lax.Precision.HIGHEST)
    meta = jnp.concatenate([slot_member, slot_weight], axis=2).astype(jnp.bfloat16)
    both = jnp.stack([tokens, out_grad], axis=1)
    sent = jnp.einsum(
        "gjt,tcd->gjcd", placed_rows, both, preferred_element_type=f32
    ).astype(jnp.bfloat16)
    pad = jnp.zeros((group_count, slots, 128 - 2 * per_group), jnp.bfloat16)
    packed = jnp.concatenate([sent.reshape(group_count, slots, 2 * width), meta, pad], axis=2)
    arrived_all = lax.all_to_all(packed, "group", split_axis=0, concat_axis=0, tiled=True)
    arrived = arrived_all[:, :, : 2 * width].reshape(group_count, slots, 2, width)
    arrived_meta = arrived_all[:, :, 2 * width : 2 * width + 2 * per_group].astype(f32)

    rows = arrived.reshape(-1, 2, width)
    arr_x = rows[:, 0]
    arr_dy = rows[:, 1]
    flat_meta = arrived_meta.reshape(-1, 2 * per_group)
    arr_members = flat_meta[:, :per_group].astype(jnp.int32)
    arr_weights = flat_meta[:, per_group:]
    member_ids = jnp.arange(experts_here, dtype=jnp.int32)
    matching = (arr_members[:, :, None] == member_ids[None, None, :]).astype(jnp.int32)
    flags = jnp.sum(matching, axis=1)
    rank = jnp.cumsum(flags, axis=0) - 1
    kept = (flags > 0) & (rank < capacity)
    cap_ids = jnp.arange(capacity, dtype=jnp.int32)
    sel = kept.T[:, None, :] & (rank.T[:, None, :] == cap_ids[None, :, None])
    sel_b = sel.astype(jnp.bfloat16)
    chooser = sel_b[:, :, :, None] * jnp.transpose(matching, (2, 0, 1))[:, None, :, :].astype(
        jnp.bfloat16
    )
    w_member = jnp.sum(matching.astype(f32) * arr_weights[:, :, None], axis=1)
    w_slot = jnp.einsum("msr,rm->ms", sel.astype(f32), w_member, precision=lax.Precision.HIGHEST)
    sel_2 = jnp.repeat(sel_b, 2, axis=0)
    w_slot_2 = jnp.repeat(w_slot, 2, axis=0)
    buf_x = jnp.einsum("msr,rd->msd", sel_2, arr_x, preferred_element_type=f32).astype(
        jnp.bfloat16
    )
    buf_dy = jnp.einsum("msr,rd->msd", sel_2, arr_dy, preferred_element_type=f32)
    buf_scaled = (w_slot_2[:, :, None] * buf_dy).astype(jnp.bfloat16)

    w_gate = gate_weight[0]
    w_up = up_weight[0]
    w_down = down_weight[0]
    inputs_here = to_owners(buf_x)
    gate, lifted, hidden, partial_value = expert_forward(inputs_here, w_gate, w_up, w_down)
    grads_here = to_owners(buf_scaled)
    partial_value, grads_here = lax.optimization_barrier(
        (partial_value.astype(jnp.bfloat16), grads_here)
    )
    outputs = from_owners(partial_value, experts_here)
    grad_gate, grad_up, grad_down, input_part = expert_backward(
        inputs_here, grads_here, gate, lifted, hidden, w_gate, w_up, w_down
    )
    input_part, grad_gate, grad_up, grad_down, outputs = lax.optimization_barrier(
        (input_part.astype(jnp.bfloat16), grad_gate, grad_up, grad_down, outputs)
    )
    input_grads = from_owners(input_part, experts_here)

    out_pair = jnp.einsum("msri,msd->rid", chooser, outputs, preferred_element_type=f32)
    in_pair = jnp.einsum("msri,msd->rid", chooser, input_grads, preferred_element_type=f32)
    group_sum = jnp.sum(arr_weights[:, :, None] * out_pair, axis=1).astype(jnp.bfloat16)
    group_grad = jnp.sum(in_pair, axis=1).astype(jnp.bfloat16)
    pair_dw = jnp.sum(arr_dy.astype(f32)[:, None, :] * out_pair, axis=2).astype(jnp.bfloat16)
    back = jnp.concatenate(
        [
            group_sum.reshape(group_count, slots, width),
            group_grad.reshape(group_count, slots, width),
            pair_dw.reshape(group_count, slots, per_group),
            jnp.zeros((group_count, slots, 128 - per_group), jnp.bfloat16),
        ],
        axis=2,
    )
    back_all = lax.all_to_all(back, "group", split_axis=0, concat_axis=0, tiled=True)
    came_back = back_all[:, :, : 2 * width].reshape(group_count, slots, 2, width)
    dw_back = back_all[:, :, 2 * width : 2 * width + per_group]

    per_token = jnp.einsum("gjt,gjcd->tcd", placed_rows, came_back, preferred_element_type=f32)
    mixed = per_token[:, 0].astype(jnp.bfloat16)
    token_grad = per_token[:, 1].astype(jnp.bfloat16)
    dw_token = jnp.einsum(
        "gjt,gji->tgi", placed_f, dw_back.astype(f32), precision=lax.Precision.HIGHEST
    )
    weight_grad = jnp.sum(sel_tki.astype(f32) * dw_token[:, None, :, :], axis=(2, 3)).astype(
        jnp.bfloat16
    )
    return (mixed, token_grad, weight_grad, grad_gate[None], grad_up[None], grad_down[None])


def solution(mesh):
    return jax.shard_map(
        local,
        mesh=mesh,
        in_specs=(
            P(("group", "local"), None),
            P(("group", "local"), None, None),
            P(("group", "local"), None, None),
            P(("group", "local"), None, None),
            P(("group", "local"), None),
            P(("group", "local"), None),
            P(("group", "local"), None),
            P(("group", "local"), None),
        ),
        out_specs=(
            P(("group", "local"), None),
            P(("group", "local"), None),
            P(("group", "local"), None),
            P(("group", "local"), None, None),
            P(("group", "local"), None, None),
            P(("group", "local"), None, None),
        ),
        check_vma=False,
    )
```

```python
import jax
import jax.numpy as jnp
from jax import lax
from jax.sharding import PartitionSpec as P

TOPK = 8
GLIM = 4


def to_owners(doubled):
    width = doubled.shape[-1]
    arrived = lax.all_to_all(doubled, "local", split_axis=0, concat_axis=0, tiled=True)
    return arrived.reshape(-1, width)


def from_owners(partial_value, experts_here):
    width = partial_value.shape[1]
    rounded = partial_value.astype(jnp.bfloat16).reshape(2 * experts_here, -1, width)
    arrived = lax.all_to_all(rounded, "local", split_axis=0, concat_axis=0, tiled=True)
    paired = arrived.reshape(experts_here, 2, -1, width)
    return (paired[:, 0].astype(jnp.float32) + paired[:, 1].astype(jnp.float32)).astype(
        jnp.bfloat16
    )


def expert_forward(inputs, w_gate, w_up, w_down):
    gate = jnp.dot(inputs, w_gate, preferred_element_type=jnp.float32)
    lifted = jnp.dot(inputs, w_up, preferred_element_type=jnp.float32)
    hidden = (gate * jax.nn.sigmoid(gate) * lifted).astype(jnp.bfloat16)
    partial_value = jnp.dot(hidden, w_down, preferred_element_type=jnp.float32)
    return (gate, lifted, hidden, partial_value)


def expert_backward(inputs, scaled, gate, lifted, hidden, w_gate, w_up, w_down):
    contract_last = (((1,), (1,)), ((), ()))
    contract_first = (((0,), (0,)), ((), ()))
    dhidden = lax.dot_general(scaled, w_down, contract_last, preferred_element_type=jnp.float32)
    grad_down = lax.dot_general(
        hidden, scaled, contract_first, preferred_element_type=jnp.float32
    ).astype(jnp.bfloat16)
    sig = jax.nn.sigmoid(gate)
    dgate = (dhidden * lifted * sig * (1.0 + gate * (1.0 - sig))).astype(jnp.bfloat16)
    dlift = (dhidden * gate * sig).astype(jnp.bfloat16)
    grad_gate = lax.dot_general(
        inputs, dgate, contract_first, preferred_element_type=jnp.float32
    ).astype(jnp.bfloat16)
    grad_up = lax.dot_general(
        inputs, dlift, contract_first, preferred_element_type=jnp.float32
    ).astype(jnp.bfloat16)
    input_part = lax.dot_general(
        dgate, w_gate, contract_last, preferred_element_type=jnp.float32
    ) + lax.dot_general(dlift, w_up, contract_last, preferred_element_type=jnp.float32)
    return (grad_gate, grad_up, grad_down, input_part)


def local(
    tokens, gate_weight, up_weight, down_weight, out_grad, group_list, expert_pick, route_weight
):
    tok_count, width = tokens.shape
    group_count = lax.axis_size("group")
    experts_here = lax.axis_size("local") // 2
    capacity = 16 * tok_count // experts_here
    per_group = TOPK // GLIM
    slots = tok_count // 2
    f32 = jnp.float32

    list_slot = expert_pick // experts_here
    member = expert_pick % experts_here
    pick_group = jnp.take_along_axis(group_list, list_slot, axis=1)
    group_ids = jnp.arange(group_count, dtype=jnp.int32)
    hit_group = (pick_group[:, :, None] == group_ids[None, None, :]).astype(jnp.int32)
    order = jnp.cumsum(hit_group, axis=1) - 1
    ordinal = jnp.sum(order * hit_group, axis=2)
    ord_ids = jnp.arange(per_group, dtype=jnp.int32)
    hit_ord = (ordinal[:, :, None] == ord_ids[None, None, :]).astype(jnp.int32)
    sel_tki = hit_group[:, :, :, None] * hit_ord[:, :, None, :]
    member_list = jnp.sum(sel_tki * member[:, :, None, None], axis=1)
    weight_list = jnp.sum(sel_tki.astype(f32) * route_weight.astype(f32)[:, :, None, None], axis=1)
    listed = jnp.sum((group_list[:, :, None] == group_ids[None, None, :]).astype(jnp.int32), axis=1)
    running = jnp.cumsum(listed, axis=0) - 1
    slot_ids = jnp.arange(slots, dtype=jnp.int32)
    placed = (listed.T[:, None, :] > 0) & (running.T[:, None, :] == slot_ids[None, :, None])
    placed_rows = placed.astype(jnp.bfloat16)
    placed_f = placed.astype(f32)
    occupied = jnp.sum(placed.astype(jnp.int32), axis=2)
    slot_member = jnp.einsum("gjt,tgi->gji", placed_f, member_list.astype(f32)) + (
        experts_here * (1 - occupied)
    ).astype(f32)[:, :, None]
    slot_weight = jnp.einsum("gjt,tgi->gji", placed_f, weight_list, precision=lax.Precision.HIGHEST)
    meta = jnp.concatenate([slot_member, slot_weight], axis=2).astype(jnp.bfloat16)
    sent_x = jnp.einsum("gjt,td->gjd", placed_rows, tokens, preferred_element_type=f32)
    sent_dy = jnp.einsum("gjt,td->gjd", placed_rows, out_grad, preferred_element_type=f32)
    pad = jnp.zeros((group_count, slots, 128 - 2 * per_group), jnp.bfloat16)
    packed = jnp.concatenate(
        [sent_x.astype(jnp.bfloat16), sent_dy.astype(jnp.bfloat16), meta, pad], axis=2
    )
    arrived_all = lax.all_to_all(packed, "group", split_axis=0, concat_axis=0, tiled=True)
    arrived_meta = arrived_all[:, :, 2 * width : 2 * width + 2 * per_group].astype(f32)

    arr_x = arrived_all[:, :, :width].reshape(-1, width)
    arr_dy = arrived_all[:, :, width : 2 * width].reshape(-1, width)
    flat_meta = arrived_meta.reshape(-1, 2 * per_group)
    arr_members = flat_meta[:, :per_group].astype(jnp.int32)
    arr_weights = flat_meta[:, per_group:]
    member_ids = jnp.arange(experts_here, dtype=jnp.int32)
    matching = (arr_members[:, :, None] == member_ids[None, None, :]).astype(jnp.int32)
    flags = jnp.sum(matching, axis=1)
    rank = jnp.cumsum(flags, axis=0) - 1
    kept = (flags > 0) & (rank < capacity)
    cap_ids = jnp.arange(capacity, dtype=jnp.int32)
    sel = kept.T[:, None, :] & (rank.T[:, None, :] == cap_ids[None, :, None])
    sel_b = sel.astype(jnp.bfloat16)
    chooser = sel_b[:, :, :, None] * jnp.transpose(matching, (2, 0, 1))[:, None, :, :].astype(
        jnp.bfloat16
    )
    w_member = jnp.sum(matching.astype(f32) * arr_weights[:, :, None], axis=1)
    w_slot = jnp.einsum("msr,rm->ms", sel.astype(f32), w_member, precision=lax.Precision.HIGHEST)
    sel_2 = jnp.repeat(sel_b, 2, axis=0)
    w_slot_2 = jnp.repeat(w_slot, 2, axis=0)
    buf_x = jnp.einsum("msr,rd->msd", sel_2, arr_x, preferred_element_type=f32).astype(
        jnp.bfloat16
    )
    buf_dy = jnp.einsum("msr,rd->msd", sel_2, arr_dy, preferred_element_type=f32)
    buf_scaled = (w_slot_2[:, :, None] * buf_dy).astype(jnp.bfloat16)

    w_gate = gate_weight[0]
    w_up = up_weight[0]
    w_down = down_weight[0]
    inputs_here = to_owners(buf_x)
    gate, lifted, hidden, partial_value = expert_forward(inputs_here, w_gate, w_up, w_down)
    grads_here = to_owners(buf_scaled)
    partial_value, grads_here = lax.optimization_barrier(
        (partial_value.astype(jnp.bfloat16), grads_here)
    )
    outputs = from_owners(partial_value, experts_here)
    grad_gate, grad_up, grad_down, input_part = expert_backward(
        inputs_here, grads_here, gate, lifted, hidden, w_gate, w_up, w_down
    )
    input_part, grad_gate, grad_up, grad_down, outputs = lax.optimization_barrier(
        (input_part.astype(jnp.bfloat16), grad_gate, grad_up, grad_down, outputs)
    )
    input_grads = from_owners(input_part, experts_here)

    out_pair = jnp.einsum("msri,msd->rid", chooser, outputs, preferred_element_type=f32)
    in_pair = jnp.einsum("msri,msd->rid", chooser, input_grads, preferred_element_type=f32)
    group_sum = jnp.sum(arr_weights[:, :, None] * out_pair, axis=1).astype(jnp.bfloat16)
    group_grad = jnp.sum(in_pair, axis=1).astype(jnp.bfloat16)
    pair_dw = jnp.sum(arr_dy.astype(f32)[:, None, :] * out_pair, axis=2).astype(jnp.bfloat16)
    back = jnp.concatenate(
        [
            group_sum.reshape(group_count, slots, width),
            group_grad.reshape(group_count, slots, width),
            pair_dw.reshape(group_count, slots, per_group),
            jnp.zeros((group_count, slots, 128 - per_group), jnp.bfloat16),
        ],
        axis=2,
    )
    back_all = lax.all_to_all(back, "group", split_axis=0, concat_axis=0, tiled=True)
    dw_back = back_all[:, :, 2 * width : 2 * width + per_group]

    mixed = jnp.einsum(
        "gjt,gjd->td", placed_rows, back_all[:, :, :width], preferred_element_type=f32
    ).astype(jnp.bfloat16)
    token_grad = jnp.einsum(
        "gjt,gjd->td", placed_rows, back_all[:, :, width : 2 * width], preferred_element_type=f32
    ).astype(jnp.bfloat16)
    dw_token = jnp.einsum(
        "gjt,gji->tgi", placed_f, dw_back.astype(f32), precision=lax.Precision.HIGHEST
    )
    weight_grad = jnp.sum(sel_tki.astype(f32) * dw_token[:, None, :, :], axis=(2, 3)).astype(
        jnp.bfloat16
    )
    return (mixed, token_grad, weight_grad, grad_gate[None], grad_up[None], grad_down[None])


def solution(mesh):
    return jax.shard_map(
        local,
        mesh=mesh,
        in_specs=(
            P(("group", "local"), None),
            P(("group", "local"), None, None),
            P(("group", "local"), None, None),
            P(("group", "local"), None, None),
            P(("group", "local"), None),
            P(("group", "local"), None),
            P(("group", "local"), None),
            P(("group", "local"), None),
        ),
        out_specs=(
            P(("group", "local"), None),
            P(("group", "local"), None),
            P(("group", "local"), None),
            P(("group", "local"), None, None),
            P(("group", "local"), None, None),
            P(("group", "local"), None, None),
        ),
        check_vma=False,
    )
```

```python
import jax
import jax.numpy as jnp
from jax import lax
from jax.sharding import PartitionSpec as P

TOPK = 8
GLIM = 4


def to_owners(doubled):
    width = doubled.shape[-1]
    arrived = lax.all_to_all(doubled, "local", split_axis=0, concat_axis=0, tiled=True)
    return arrived.reshape(-1, width)


def from_owners(partial_value, experts_here):
    width = partial_value.shape[1]
    rounded = partial_value.astype(jnp.bfloat16).reshape(2 * experts_here, -1, width)
    arrived = lax.all_to_all(rounded, "local", split_axis=0, concat_axis=0, tiled=True)
    paired = arrived.reshape(experts_here, 2, -1, width)
    return (paired[:, 0].astype(jnp.float32) + paired[:, 1].astype(jnp.float32)).astype(
        jnp.bfloat16
    )


def expert_forward(inputs, w_gate, w_up, w_down):
    gate = jnp.dot(inputs, w_gate, preferred_element_type=jnp.float32)
    lifted = jnp.dot(inputs, w_up, preferred_element_type=jnp.float32)
    hidden = (gate * jax.nn.sigmoid(gate) * lifted).astype(jnp.bfloat16)
    partial_value = jnp.dot(hidden, w_down, preferred_element_type=jnp.float32)
    return (gate, lifted, hidden, partial_value)


def expert_backward(inputs, scaled, gate, lifted, hidden, w_gate, w_up, w_down):
    contract_last = (((1,), (1,)), ((), ()))
    contract_first = (((0,), (0,)), ((), ()))
    dhidden = lax.dot_general(scaled, w_down, contract_last, preferred_element_type=jnp.float32)
    grad_down = lax.dot_general(
        hidden, scaled, contract_first, preferred_element_type=jnp.float32
    ).astype(jnp.bfloat16)
    sig = jax.nn.sigmoid(gate)
    dgate = (dhidden * lifted * sig * (1.0 + gate * (1.0 - sig))).astype(jnp.bfloat16)
    dlift = (dhidden * gate * sig).astype(jnp.bfloat16)
    grad_gate = lax.dot_general(
        inputs, dgate, contract_first, preferred_element_type=jnp.float32
    ).astype(jnp.bfloat16)
    grad_up = lax.dot_general(
        inputs, dlift, contract_first, preferred_element_type=jnp.float32
    ).astype(jnp.bfloat16)
    input_part = lax.dot_general(
        dgate, w_gate, contract_last, preferred_element_type=jnp.float32
    ) + lax.dot_general(dlift, w_up, contract_last, preferred_element_type=jnp.float32)
    return (grad_gate, grad_up, grad_down, input_part)


def local(
    tokens, gate_weight, up_weight, down_weight, out_grad, group_list, expert_pick, route_weight
):
    tok_count, width = tokens.shape
    group_count = lax.axis_size("group")
    experts_here = lax.axis_size("local") // 2
    capacity = 16 * tok_count // experts_here
    per_group = TOPK // GLIM
    slots = tok_count // 2
    f32 = jnp.float32

    list_slot = expert_pick // experts_here
    member = expert_pick % experts_here
    pick_group = jnp.take_along_axis(group_list, list_slot, axis=1)
    group_ids = jnp.arange(group_count, dtype=jnp.int32)
    hit_group = (pick_group[:, :, None] == group_ids[None, None, :]).astype(jnp.int32)
    order = jnp.cumsum(hit_group, axis=1) - 1
    ordinal = jnp.sum(order * hit_group, axis=2)
    ord_ids = jnp.arange(per_group, dtype=jnp.int32)
    hit_ord = (ordinal[:, :, None] == ord_ids[None, None, :]).astype(jnp.int32)
    sel_tki = hit_group[:, :, :, None] * hit_ord[:, :, None, :]
    member_list = jnp.sum(sel_tki * member[:, :, None, None], axis=1)
    weight_list = jnp.sum(sel_tki.astype(f32) * route_weight.astype(f32)[:, :, None, None], axis=1)
    listed = jnp.sum((group_list[:, :, None] == group_ids[None, None, :]).astype(jnp.int32), axis=1)
    running = jnp.cumsum(listed, axis=0) - 1
    slot_ids = jnp.arange(slots, dtype=jnp.int32)
    placed = (listed.T[:, None, :] > 0) & (running.T[:, None, :] == slot_ids[None, :, None])
    placed_rows = placed.astype(jnp.bfloat16)
    placed_f = placed.astype(f32)
    token_meta = jnp.concatenate(
        [
            (member_list + 1).astype(f32).reshape(tok_count, group_count * per_group),
            weight_list.reshape(tok_count, group_count * per_group),
            jnp.zeros((tok_count, 128 - 2 * group_count * per_group), f32),
        ],
        axis=1,
    ).astype(jnp.bfloat16)
    token_all = jnp.concatenate([tokens, out_grad, token_meta], axis=1)
    packed = jnp.einsum(
        "gjt,tc->gjc", placed_rows, token_all, preferred_element_type=f32
    ).astype(jnp.bfloat16)
    arrived_all = lax.all_to_all(packed, "group", split_axis=0, concat_axis=0, tiled=True)
    me_group = lax.axis_index("group")
    meta_all = arrived_all[:, :, 2 * width :].astype(f32)
    own = (jnp.arange(128, dtype=jnp.int32) // per_group) == me_group
    own = own & (jnp.arange(128) < group_count * per_group)
    own_w = (
        ((jnp.arange(128, dtype=jnp.int32) - group_count * per_group) // per_group) == me_group
    ) & (jnp.arange(128) >= group_count * per_group) & (
        jnp.arange(128) < 2 * group_count * per_group
    )
    pos = jnp.arange(128, dtype=jnp.int32) % per_group
    pick_pos = (pos[:, None] == jnp.arange(per_group, dtype=jnp.int32)[None, :]).astype(f32)
    meta_members = jnp.einsum(
        "gjc,ci->gji", meta_all, own.astype(f32)[:, None] * pick_pos,
        precision=lax.Precision.HIGHEST,
    ) - 1.0
    meta_weights = jnp.einsum(
        "gjc,ci->gji", meta_all, own_w.astype(f32)[:, None] * pick_pos,
        precision=lax.Precision.HIGHEST,
    )
    arrived_meta = jnp.concatenate([meta_members, meta_weights], axis=2)

    arr_x = arrived_all[:, :, :width].reshape(-1, width)
    arr_dy = arrived_all[:, :, width : 2 * width].reshape(-1, width)
    flat_meta = arrived_meta.reshape(-1, 2 * per_group)
    arr_members = jnp.round(flat_meta[:, :per_group]).astype(jnp.int32)
    arr_weights = flat_meta[:, per_group:]
    member_ids = jnp.arange(experts_here, dtype=jnp.int32)
    matching = (arr_members[:, :, None] == member_ids[None, None, :]).astype(jnp.int32)
    flags = jnp.sum(matching, axis=1)
    rank = jnp.cumsum(flags, axis=0) - 1
    kept = (flags > 0) & (rank < capacity)
    cap_ids = jnp.arange(capacity, dtype=jnp.int32)
    sel = kept.T[:, None, :] & (rank.T[:, None, :] == cap_ids[None, :, None])
    sel_b = sel.astype(jnp.bfloat16)
    chooser = sel_b[:, :, :, None] * jnp.transpose(matching, (2, 0, 1))[:, None, :, :].astype(
        jnp.bfloat16
    )
    w_member = jnp.sum(matching.astype(f32) * arr_weights[:, :, None], axis=1)
    w_slot = jnp.einsum("msr,rm->ms", sel.astype(f32), w_member, precision=lax.Precision.HIGHEST)
    sel_2 = jnp.repeat(sel_b, 2, axis=0)
    w_slot_2 = jnp.repeat(w_slot, 2, axis=0)
    buf_x = jnp.einsum("msr,rd->msd", sel_2, arr_x, preferred_element_type=f32).astype(
        jnp.bfloat16
    )
    buf_dy = jnp.einsum("msr,rd->msd", sel_2, arr_dy, preferred_element_type=f32)
    buf_scaled = (w_slot_2[:, :, None] * buf_dy).astype(jnp.bfloat16)

    w_gate = gate_weight[0]
    w_up = up_weight[0]
    w_down = down_weight[0]
    inputs_here = to_owners(buf_x)
    gate, lifted, hidden, partial_value = expert_forward(inputs_here, w_gate, w_up, w_down)
    grads_here = to_owners(buf_scaled)
    partial_value, grads_here = lax.optimization_barrier(
        (partial_value.astype(jnp.bfloat16), grads_here)
    )
    outputs = lax.all_to_all(
        partial_value.reshape(2 * experts_here, capacity, width), "local", split_axis=0,
        concat_axis=0, tiled=True,
    )
    grad_gate, grad_up, grad_down, input_part = expert_backward(
        inputs_here, grads_here, gate, lifted, hidden, w_gate, w_up, w_down
    )
    input_part, grad_gate, grad_up, grad_down, outputs = lax.optimization_barrier(
        (input_part.astype(jnp.bfloat16), grad_gate, grad_up, grad_down, outputs)
    )
    input_grads = lax.all_to_all(
        input_part.reshape(2 * experts_here, capacity, width), "local", split_axis=0,
        concat_axis=0, tiled=True,
    )

    chooser_2 = jnp.repeat(chooser, 2, axis=0)
    out_pair = jnp.einsum("msri,msd->rid", chooser_2, outputs, preferred_element_type=f32)
    in_pair = jnp.einsum("msri,msd->rid", chooser_2, input_grads, preferred_element_type=f32)
    group_sum = jnp.sum(arr_weights[:, :, None] * out_pair, axis=1).astype(jnp.bfloat16)
    group_grad = jnp.sum(in_pair, axis=1).astype(jnp.bfloat16)
    pair_dw = jnp.sum(arr_dy.astype(f32)[:, None, :] * out_pair, axis=2).astype(jnp.bfloat16)
    back = jnp.concatenate(
        [
            group_sum.reshape(group_count, slots, width),
            group_grad.reshape(group_count, slots, width),
            pair_dw.reshape(group_count, slots, per_group),
            jnp.zeros((group_count, slots, 128 - per_group), jnp.bfloat16),
        ],
        axis=2,
    )
    back_all = lax.all_to_all(back, "group", split_axis=0, concat_axis=0, tiled=True)
    dw_back = back_all[:, :, 2 * width : 2 * width + per_group]

    mixed = jnp.einsum(
        "gjt,gjd->td", placed_rows, back_all[:, :, :width], preferred_element_type=f32
    ).astype(jnp.bfloat16)
    token_grad = jnp.einsum(
        "gjt,gjd->td", placed_rows, back_all[:, :, width : 2 * width], preferred_element_type=f32
    ).astype(jnp.bfloat16)
    dw_token = jnp.einsum(
        "gjt,gji->tgi", placed_f, dw_back.astype(f32), precision=lax.Precision.HIGHEST
    )
    weight_grad = jnp.sum(sel_tki.astype(f32) * dw_token[:, None, :, :], axis=(2, 3)).astype(
        jnp.bfloat16
    )
    return (mixed, token_grad, weight_grad, grad_gate[None], grad_up[None], grad_down[None])


def solution(mesh):
    return jax.shard_map(
        local,
        mesh=mesh,
        in_specs=(
            P(("group", "local"), None),
            P(("group", "local"), None, None),
            P(("group", "local"), None, None),
            P(("group", "local"), None, None),
            P(("group", "local"), None),
            P(("group", "local"), None),
            P(("group", "local"), None),
            P(("group", "local"), None),
        ),
        out_specs=(
            P(("group", "local"), None),
            P(("group", "local"), None),
            P(("group", "local"), None),
            P(("group", "local"), None, None),
            P(("group", "local"), None, None),
            P(("group", "local"), None, None),
        ),
        check_vma=False,
    )
```

```python
import jax
import jax.numpy as jnp
from jax import lax
from jax.sharding import PartitionSpec as P

TOPK = 8
GLIM = 4


def to_owners(doubled):
    width = doubled.shape[-1]
    arrived = lax.all_to_all(doubled, "local", split_axis=0, concat_axis=0, tiled=True)
    return arrived.reshape(-1, width)


def from_owners(partial_value, experts_here):
    width = partial_value.shape[1]
    rounded = partial_value.astype(jnp.bfloat16).reshape(2 * experts_here, -1, width)
    arrived = lax.all_to_all(rounded, "local", split_axis=0, concat_axis=0, tiled=True)
    paired = arrived.reshape(experts_here, 2, -1, width)
    return (paired[:, 0].astype(jnp.float32) + paired[:, 1].astype(jnp.float32)).astype(
        jnp.bfloat16
    )


def expert_forward(inputs, w_gate, w_up, w_down):
    gate = jnp.dot(inputs, w_gate, preferred_element_type=jnp.float32)
    lifted = jnp.dot(inputs, w_up, preferred_element_type=jnp.float32)
    hidden = (gate * jax.nn.sigmoid(gate) * lifted).astype(jnp.bfloat16)
    partial_value = jnp.dot(hidden, w_down, preferred_element_type=jnp.float32)
    return (gate, lifted, hidden, partial_value)


def expert_backward(inputs, scaled, gate, lifted, hidden, w_gate, w_up, w_down):
    contract_last = (((1,), (1,)), ((), ()))
    contract_first = (((0,), (0,)), ((), ()))
    dhidden = lax.dot_general(scaled, w_down, contract_last, preferred_element_type=jnp.float32)
    grad_down = lax.dot_general(
        hidden, scaled, contract_first, preferred_element_type=jnp.float32
    ).astype(jnp.bfloat16)
    sig = jax.nn.sigmoid(gate)
    dgate = (dhidden * lifted * sig * (1.0 + gate * (1.0 - sig))).astype(jnp.bfloat16)
    dlift = (dhidden * gate * sig).astype(jnp.bfloat16)
    grad_gate = lax.dot_general(
        inputs, dgate, contract_first, preferred_element_type=jnp.float32
    ).astype(jnp.bfloat16)
    grad_up = lax.dot_general(
        inputs, dlift, contract_first, preferred_element_type=jnp.float32
    ).astype(jnp.bfloat16)
    input_part = lax.dot_general(
        dgate, w_gate, contract_last, preferred_element_type=jnp.float32
    ) + lax.dot_general(dlift, w_up, contract_last, preferred_element_type=jnp.float32)
    return (grad_gate, grad_up, grad_down, input_part)


def local(
    tokens, gate_weight, up_weight, down_weight, out_grad, group_list, expert_pick, route_weight
):
    tok_count, width = tokens.shape
    group_count = lax.axis_size("group")
    experts_here = lax.axis_size("local") // 2
    capacity = 16 * tok_count // experts_here
    per_group = TOPK // GLIM
    slots = tok_count // 2
    f32 = jnp.float32

    list_slot = expert_pick // experts_here
    member = expert_pick % experts_here
    pick_group = jnp.take_along_axis(group_list, list_slot, axis=1)
    group_ids = jnp.arange(group_count, dtype=jnp.int32)
    hit_group = (pick_group[:, :, None] == group_ids[None, None, :]).astype(jnp.int32)
    order = jnp.cumsum(hit_group, axis=1) - 1
    ordinal = jnp.sum(order * hit_group, axis=2)
    ord_ids = jnp.arange(per_group, dtype=jnp.int32)
    hit_ord = (ordinal[:, :, None] == ord_ids[None, None, :]).astype(jnp.int32)
    sel_tki = hit_group[:, :, :, None] * hit_ord[:, :, None, :]
    member_list = jnp.sum(sel_tki * member[:, :, None, None], axis=1)
    weight_list = jnp.sum(sel_tki.astype(f32) * route_weight.astype(f32)[:, :, None, None], axis=1)
    listed = jnp.sum((group_list[:, :, None] == group_ids[None, None, :]).astype(jnp.int32), axis=1)
    running = jnp.cumsum(listed, axis=0) - 1
    slot_ids = jnp.arange(slots, dtype=jnp.int32)
    placed = (listed.T[:, None, :] > 0) & (running.T[:, None, :] == slot_ids[None, :, None])
    placed_rows = placed.astype(jnp.bfloat16)
    placed_f = placed.astype(f32)
    token_meta = jnp.concatenate(
        [
            (member_list + 1).astype(f32).reshape(tok_count, group_count * per_group),
            weight_list.reshape(tok_count, group_count * per_group),
            jnp.zeros((tok_count, 128 - 2 * group_count * per_group), f32),
        ],
        axis=1,
    ).astype(jnp.bfloat16)
    token_all = jnp.concatenate([tokens, out_grad, token_meta], axis=1)
    packed = jnp.einsum(
        "gjt,tc->gjc", placed_rows, token_all, preferred_element_type=f32
    ).astype(jnp.bfloat16)
    arrived_all = lax.all_to_all(packed, "group", split_axis=0, concat_axis=0, tiled=True)
    me_group = lax.axis_index("group")
    meta_all = arrived_all[:, :, 2 * width :].astype(f32)
    own = (jnp.arange(128, dtype=jnp.int32) // per_group) == me_group
    own = own & (jnp.arange(128) < group_count * per_group)
    own_w = (
        ((jnp.arange(128, dtype=jnp.int32) - group_count * per_group) // per_group) == me_group
    ) & (jnp.arange(128) >= group_count * per_group) & (
        jnp.arange(128) < 2 * group_count * per_group
    )
    pos = jnp.arange(128, dtype=jnp.int32) % per_group
    pick_pos = (pos[:, None] == jnp.arange(per_group, dtype=jnp.int32)[None, :]).astype(f32)
    meta_members = jnp.einsum(
        "gjc,ci->gji", meta_all, own.astype(f32)[:, None] * pick_pos,
        precision=lax.Precision.HIGHEST,
    ) - 1.0
    meta_weights = jnp.einsum(
        "gjc,ci->gji", meta_all, own_w.astype(f32)[:, None] * pick_pos,
        precision=lax.Precision.HIGHEST,
    )
    arrived_meta = jnp.concatenate([meta_members, meta_weights], axis=2)

    arr_x = arrived_all[:, :, :width].reshape(-1, width)
    arr_dy = arrived_all[:, :, width : 2 * width].reshape(-1, width)
    flat_meta = arrived_meta.reshape(-1, 2 * per_group)
    arr_members = jnp.round(flat_meta[:, :per_group]).astype(jnp.int32)
    arr_weights = flat_meta[:, per_group:]
    member_ids = jnp.arange(experts_here, dtype=jnp.int32)
    matching = (arr_members[:, :, None] == member_ids[None, None, :]).astype(jnp.int32)
    flags = jnp.sum(matching, axis=1)
    rank = jnp.cumsum(flags, axis=0) - 1
    kept = (flags > 0) & (rank < capacity)
    cap_ids = jnp.arange(capacity, dtype=jnp.int32)
    sel = kept.T[:, None, :] & (rank.T[:, None, :] == cap_ids[None, :, None])
    sel_b = sel.astype(jnp.bfloat16)
    chooser = sel_b[:, :, :, None] * jnp.transpose(matching, (2, 0, 1))[:, None, :, :].astype(
        jnp.bfloat16
    )
    w_member = jnp.sum(matching.astype(f32) * arr_weights[:, :, None], axis=1)
    w_slot = jnp.einsum("msr,rm->ms", sel.astype(f32), w_member, precision=lax.Precision.HIGHEST)
    sel_2 = jnp.repeat(sel_b, 2, axis=0)
    w_slot_2 = jnp.repeat(w_slot, 2, axis=0)
    buf_x = jnp.einsum("msr,rd->msd", sel_2, arr_x, preferred_element_type=f32).astype(
        jnp.bfloat16
    )
    buf_dy = jnp.einsum("msr,rd->msd", sel_2, arr_dy, preferred_element_type=f32)
    buf_scaled = (w_slot_2[:, :, None] * buf_dy).astype(jnp.bfloat16)

    w_gate = gate_weight[0]
    w_up = up_weight[0]
    w_down = down_weight[0]
    inputs_here = to_owners(buf_x)
    gate, lifted, hidden, partial_value = expert_forward(inputs_here, w_gate, w_up, w_down)
    grads_here = to_owners(buf_scaled)
    partial_value, grads_here = lax.optimization_barrier(
        (partial_value.astype(jnp.bfloat16), grads_here)
    )
    outputs = lax.all_to_all(
        partial_value.reshape(2 * experts_here, capacity, width), "local", split_axis=0,
        concat_axis=0, tiled=True,
    )
    grad_gate, grad_up, grad_down, input_part = expert_backward(
        inputs_here, grads_here, gate, lifted, hidden, w_gate, w_up, w_down
    )
    input_part, grad_gate, grad_up, grad_down, outputs = lax.optimization_barrier(
        (input_part.astype(jnp.bfloat16), grad_gate, grad_up, grad_down, outputs)
    )
    input_grads = lax.all_to_all(
        input_part.reshape(2 * experts_here, capacity, width), "local", split_axis=0,
        concat_axis=0, tiled=True,
    )

    chooser_2 = jnp.repeat(chooser, 2, axis=0)
    out_pair = jnp.einsum("msri,msd->rid", chooser_2, outputs, preferred_element_type=f32)
    in_pair = jnp.einsum("msri,msd->rid", chooser_2, input_grads, preferred_element_type=f32)
    group_sum = jnp.sum(arr_weights[:, :, None] * out_pair, axis=1).astype(jnp.bfloat16)
    group_grad = jnp.sum(in_pair, axis=1).astype(jnp.bfloat16)
    pair_dw = jnp.sum(arr_dy.astype(f32)[:, None, :] * out_pair, axis=2).astype(jnp.bfloat16)
    fwd_back = jnp.concatenate(
        [
            group_sum.reshape(group_count, slots, width),
            pair_dw.reshape(group_count, slots, per_group),
            jnp.zeros((group_count, slots, 128 - per_group), jnp.bfloat16),
        ],
        axis=2,
    )
    me_g = lax.axis_index("group")
    shifted = [fwd_back[me_g]]
    for shift in range(1, group_count):
        piece = lax.dynamic_index_in_dim(fwd_back, (me_g + shift) % group_count, 0, False)
        perm = [(i, (i + shift) % group_count) for i in range(group_count)]
        shifted.append(lax.ppermute(piece, "group", perm))
    fwd_came = jnp.stack(shifted)
    src_of = (me_g - jnp.arange(group_count, dtype=jnp.int32)) % group_count
    placed_from = jnp.take(placed_rows, src_of, axis=0)
    grad_back = lax.all_to_all(
        group_grad.reshape(group_count, slots, width), "group", split_axis=0, concat_axis=0,
        tiled=True,
    )
    dw_back = jnp.take(fwd_came[:, :, width : width + per_group], src_of, axis=0)

    mixed = jnp.einsum(
        "gjt,gjd->td", placed_from, fwd_came[:, :, :width], preferred_element_type=f32
    ).astype(jnp.bfloat16)
    token_grad = jnp.einsum(
        "gjt,gjd->td", placed_rows, grad_back, preferred_element_type=f32
    ).astype(jnp.bfloat16)
    dw_token = jnp.einsum(
        "gjt,gji->tgi", placed_f, dw_back.astype(f32), precision=lax.Precision.HIGHEST
    )
    weight_grad = jnp.sum(sel_tki.astype(f32) * dw_token[:, None, :, :], axis=(2, 3)).astype(
        jnp.bfloat16
    )
    return (mixed, token_grad, weight_grad, grad_gate[None], grad_up[None], grad_down[None])


def solution(mesh):
    return jax.shard_map(
        local,
        mesh=mesh,
        in_specs=(
            P(("group", "local"), None),
            P(("group", "local"), None, None),
            P(("group", "local"), None, None),
            P(("group", "local"), None, None),
            P(("group", "local"), None),
            P(("group", "local"), None),
            P(("group", "local"), None),
            P(("group", "local"), None),
        ),
        out_specs=(
            P(("group", "local"), None),
            P(("group", "local"), None),
            P(("group", "local"), None),
            P(("group", "local"), None, None),
            P(("group", "local"), None, None),
            P(("group", "local"), None, None),
        ),
        check_vma=False,
    )
```

```python
import jax
import jax.numpy as jnp
from jax import lax
from jax.sharding import PartitionSpec as P

TOPK = 8
GLIM = 4


def to_owners(doubled):
    width = doubled.shape[-1]
    arrived = lax.all_to_all(doubled, "local", split_axis=0, concat_axis=0, tiled=True)
    return arrived.reshape(-1, width)


def group_exchange(payload, me_g):
    count = payload.shape[0]
    shifted = [payload[me_g]]
    for shift in range(1, count):
        piece = lax.dynamic_index_in_dim(payload, (me_g + shift) % count, 0, False)
        perm = [(i, (i + shift) % count) for i in range(count)]
        shifted.append(lax.ppermute(piece, "group", perm))
    return jnp.stack(shifted)


def expert_forward(inputs, w_gate, w_up, w_down):
    gate = jnp.dot(inputs, w_gate, preferred_element_type=jnp.float32)
    lifted = jnp.dot(inputs, w_up, preferred_element_type=jnp.float32)
    hidden = (gate * jax.nn.sigmoid(gate) * lifted).astype(jnp.bfloat16)
    partial_value = jnp.dot(hidden, w_down, preferred_element_type=jnp.float32)
    return (gate, lifted, hidden, partial_value)


def expert_backward(inputs, scaled, gate, lifted, hidden, w_gate, w_up, w_down):
    contract_last = (((1,), (1,)), ((), ()))
    contract_first = (((0,), (0,)), ((), ()))
    dhidden = lax.dot_general(scaled, w_down, contract_last, preferred_element_type=jnp.float32)
    grad_down = lax.dot_general(
        hidden, scaled, contract_first, preferred_element_type=jnp.float32
    ).astype(jnp.bfloat16)
    sig = jax.nn.sigmoid(gate)
    dgate = (dhidden * lifted * sig * (1.0 + gate * (1.0 - sig))).astype(jnp.bfloat16)
    dlift = (dhidden * gate * sig).astype(jnp.bfloat16)
    grad_gate = lax.dot_general(
        inputs, dgate, contract_first, preferred_element_type=jnp.float32
    ).astype(jnp.bfloat16)
    grad_up = lax.dot_general(
        inputs, dlift, contract_first, preferred_element_type=jnp.float32
    ).astype(jnp.bfloat16)
    input_part = lax.dot_general(
        dgate, w_gate, contract_last, preferred_element_type=jnp.float32
    ) + lax.dot_general(dlift, w_up, contract_last, preferred_element_type=jnp.float32)
    return (grad_gate, grad_up, grad_down, input_part)


def local(
    tokens, gate_weight, up_weight, down_weight, out_grad, group_list, expert_pick, route_weight
):
    tok_count, width = tokens.shape
    group_count = lax.axis_size("group")
    experts_here = lax.axis_size("local") // 2
    capacity = 16 * tok_count // experts_here
    per_group = TOPK // GLIM
    slots = tok_count // 2
    f32 = jnp.float32

    list_slot = expert_pick // experts_here
    member = expert_pick % experts_here
    pick_group = jnp.take_along_axis(group_list, list_slot, axis=1)
    group_ids = jnp.arange(group_count, dtype=jnp.int32)
    hit_group = (pick_group[:, :, None] == group_ids[None, None, :]).astype(jnp.int32)
    order = jnp.cumsum(hit_group, axis=1) - 1
    ordinal = jnp.sum(order * hit_group, axis=2)
    ord_ids = jnp.arange(per_group, dtype=jnp.int32)
    hit_ord = (ordinal[:, :, None] == ord_ids[None, None, :]).astype(jnp.int32)
    sel_tki = hit_group[:, :, :, None] * hit_ord[:, :, None, :]
    member_list = jnp.sum(sel_tki * member[:, :, None, None], axis=1)
    weight_list = jnp.sum(sel_tki.astype(f32) * route_weight.astype(f32)[:, :, None, None], axis=1)
    listed = jnp.sum((group_list[:, :, None] == group_ids[None, None, :]).astype(jnp.int32), axis=1)
    running = jnp.cumsum(listed, axis=0) - 1
    slot_ids = jnp.arange(slots, dtype=jnp.int32)
    placed = (listed.T[:, None, :] > 0) & (running.T[:, None, :] == slot_ids[None, :, None])
    placed_rows = placed.astype(jnp.bfloat16)
    placed_f = placed.astype(f32)
    token_meta = jnp.concatenate(
        [
            (member_list + 1).astype(f32).reshape(tok_count, group_count * per_group),
            weight_list.reshape(tok_count, group_count * per_group),
            jnp.zeros((tok_count, 128 - 2 * group_count * per_group), f32),
        ],
        axis=1,
    ).astype(jnp.bfloat16)
    token_all = jnp.concatenate([tokens, out_grad, token_meta], axis=1)
    packed = jnp.einsum(
        "gjt,tc->gjc", placed_rows, token_all, preferred_element_type=f32
    ).astype(jnp.bfloat16)
    me_g = lax.axis_index("group")
    src_of = (me_g - jnp.arange(group_count, dtype=jnp.int32)) % group_count
    arrived_all = jnp.take(group_exchange(packed, me_g), src_of, axis=0)
    me_group = me_g
    meta_all = arrived_all[:, :, 2 * width :].astype(f32)
    own = (jnp.arange(128, dtype=jnp.int32) // per_group) == me_group
    own = own & (jnp.arange(128) < group_count * per_group)
    own_w = (
        ((jnp.arange(128, dtype=jnp.int32) - group_count * per_group) // per_group) == me_group
    ) & (jnp.arange(128) >= group_count * per_group) & (
        jnp.arange(128) < 2 * group_count * per_group
    )
    pos = jnp.arange(128, dtype=jnp.int32) % per_group
    pick_pos = (pos[:, None] == jnp.arange(per_group, dtype=jnp.int32)[None, :]).astype(f32)
    meta_members = jnp.einsum(
        "gjc,ci->gji", meta_all, own.astype(f32)[:, None] * pick_pos,
        precision=lax.Precision.HIGHEST,
    ) - 1.0
    meta_weights = jnp.einsum(
        "gjc,ci->gji", meta_all, own_w.astype(f32)[:, None] * pick_pos,
        precision=lax.Precision.HIGHEST,
    )
    arrived_meta = jnp.concatenate([meta_members, meta_weights], axis=2)

    arr_x = arrived_all[:, :, :width].reshape(-1, width)
    arr_dy = arrived_all[:, :, width : 2 * width].reshape(-1, width)
    flat_meta = arrived_meta.reshape(-1, 2 * per_group)
    arr_members = jnp.round(flat_meta[:, :per_group]).astype(jnp.int32)
    arr_weights = flat_meta[:, per_group:]
    member_ids = jnp.arange(experts_here, dtype=jnp.int32)
    matching = (arr_members[:, :, None] == member_ids[None, None, :]).astype(jnp.int32)
    flags = jnp.sum(matching, axis=1)
    rank = jnp.cumsum(flags, axis=0) - 1
    kept = (flags > 0) & (rank < capacity)
    cap_ids = jnp.arange(capacity, dtype=jnp.int32)
    sel = kept.T[:, None, :] & (rank.T[:, None, :] == cap_ids[None, :, None])
    sel_b = sel.astype(jnp.bfloat16)
    chooser = sel_b[:, :, :, None] * jnp.transpose(matching, (2, 0, 1))[:, None, :, :].astype(
        jnp.bfloat16
    )
    w_member = jnp.sum(matching.astype(f32) * arr_weights[:, :, None], axis=1)
    w_slot = jnp.einsum("msr,rm->ms", sel.astype(f32), w_member, precision=lax.Precision.HIGHEST)
    sel_2 = jnp.repeat(sel_b, 2, axis=0)
    w_slot_2 = jnp.repeat(w_slot, 2, axis=0)
    buf_x = jnp.einsum("msr,rd->msd", sel_2, arr_x, preferred_element_type=f32).astype(
        jnp.bfloat16
    )
    buf_dy = jnp.einsum("msr,rd->msd", sel_2, arr_dy, preferred_element_type=f32)
    buf_scaled = (w_slot_2[:, :, None] * buf_dy).astype(jnp.bfloat16)

    w_gate = gate_weight[0]
    w_up = up_weight[0]
    w_down = down_weight[0]
    inputs_here = to_owners(buf_x)
    gate, lifted, hidden, partial_value = expert_forward(inputs_here, w_gate, w_up, w_down)
    grads_here = to_owners(buf_scaled)
    partial_value, grads_here = lax.optimization_barrier(
        (partial_value.astype(jnp.bfloat16), grads_here)
    )
    outputs = lax.all_to_all(
        partial_value.reshape(2 * experts_here, capacity, width), "local", split_axis=0,
        concat_axis=0, tiled=True,
    )
    grad_gate, grad_up, grad_down, input_part = expert_backward(
        inputs_here, grads_here, gate, lifted, hidden, w_gate, w_up, w_down
    )
    input_part, grad_gate, grad_up, grad_down, outputs = lax.optimization_barrier(
        (input_part.astype(jnp.bfloat16), grad_gate, grad_up, grad_down, outputs)
    )
    input_grads = lax.all_to_all(
        input_part.reshape(2 * experts_here, capacity, width), "local", split_axis=0,
        concat_axis=0, tiled=True,
    )

    chooser_2 = jnp.repeat(chooser, 2, axis=0)
    out_pair = jnp.einsum("msri,msd->rid", chooser_2, outputs, preferred_element_type=f32)
    in_pair = jnp.einsum("msri,msd->rid", chooser_2, input_grads, preferred_element_type=f32)
    group_sum = jnp.sum(arr_weights[:, :, None] * out_pair, axis=1).astype(jnp.bfloat16)
    group_grad = jnp.sum(in_pair, axis=1).astype(jnp.bfloat16)
    pair_dw = jnp.sum(arr_dy.astype(f32)[:, None, :] * out_pair, axis=2).astype(jnp.bfloat16)
    back = jnp.concatenate(
        [
            group_sum.reshape(group_count, slots, width),
            group_grad.reshape(group_count, slots, width),
            pair_dw.reshape(group_count, slots, per_group),
            jnp.zeros((group_count, slots, 128 - per_group), jnp.bfloat16),
        ],
        axis=2,
    )
    back_all = jnp.take(group_exchange(back, me_g), src_of, axis=0)
    dw_back = back_all[:, :, 2 * width : 2 * width + per_group]

    mixed = jnp.einsum(
        "gjt,gjd->td", placed_rows, back_all[:, :, :width], preferred_element_type=f32
    ).astype(jnp.bfloat16)
    token_grad = jnp.einsum(
        "gjt,gjd->td", placed_rows, back_all[:, :, width : 2 * width], preferred_element_type=f32
    ).astype(jnp.bfloat16)
    dw_token = jnp.einsum(
        "gjt,gji->tgi", placed_f, dw_back.astype(f32), precision=lax.Precision.HIGHEST
    )
    weight_grad = jnp.sum(sel_tki.astype(f32) * dw_token[:, None, :, :], axis=(2, 3)).astype(
        jnp.bfloat16
    )
    return (mixed, token_grad, weight_grad, grad_gate[None], grad_up[None], grad_down[None])


def solution(mesh):
    return jax.shard_map(
        local,
        mesh=mesh,
        in_specs=(
            P(("group", "local"), None),
            P(("group", "local"), None, None),
            P(("group", "local"), None, None),
            P(("group", "local"), None, None),
            P(("group", "local"), None),
            P(("group", "local"), None),
            P(("group", "local"), None),
            P(("group", "local"), None),
        ),
        out_specs=(
            P(("group", "local"), None),
            P(("group", "local"), None),
            P(("group", "local"), None),
            P(("group", "local"), None, None),
            P(("group", "local"), None, None),
            P(("group", "local"), None, None),
        ),
        check_vma=False,
    )
```

```python
import jax
import jax.numpy as jnp
from jax import lax
from jax.sharding import PartitionSpec as P

TOPK = 8
GLIM = 4


def to_owners(doubled):
    width = doubled.shape[-1]
    arrived = lax.all_to_all(doubled, "local", split_axis=0, concat_axis=0, tiled=True)
    return arrived.reshape(-1, width)


def expert_forward(inputs, w_gate, w_up, w_down):
    gate = jnp.dot(inputs, w_gate, preferred_element_type=jnp.float32)
    lifted = jnp.dot(inputs, w_up, preferred_element_type=jnp.float32)
    hidden = (gate * jax.nn.sigmoid(gate) * lifted).astype(jnp.bfloat16)
    partial_value = jnp.dot(hidden, w_down, preferred_element_type=jnp.float32)
    return (gate, lifted, hidden, partial_value)


def expert_backward(inputs, scaled, gate, lifted, hidden, w_gate, w_up, w_down):
    contract_last = (((1,), (1,)), ((), ()))
    contract_first = (((0,), (0,)), ((), ()))
    dhidden = lax.dot_general(scaled, w_down, contract_last, preferred_element_type=jnp.float32)
    grad_down = lax.dot_general(
        hidden, scaled, contract_first, preferred_element_type=jnp.float32
    ).astype(jnp.bfloat16)
    sig = jax.nn.sigmoid(gate)
    dgate = (dhidden * lifted * sig * (1.0 + gate * (1.0 - sig))).astype(jnp.bfloat16)
    dlift = (dhidden * gate * sig).astype(jnp.bfloat16)
    grad_gate = lax.dot_general(
        inputs, dgate, contract_first, preferred_element_type=jnp.float32
    ).astype(jnp.bfloat16)
    grad_up = lax.dot_general(
        inputs, dlift, contract_first, preferred_element_type=jnp.float32
    ).astype(jnp.bfloat16)
    input_part = lax.dot_general(
        dgate, w_gate, contract_last, preferred_element_type=jnp.float32
    ) + lax.dot_general(dlift, w_up, contract_last, preferred_element_type=jnp.float32)
    return (grad_gate, grad_up, grad_down, input_part)


def local(
    tokens, gate_weight, up_weight, down_weight, out_grad, group_list, expert_pick, route_weight
):
    tok_count, width = tokens.shape
    group_count = lax.axis_size("group")
    experts_here = lax.axis_size("local") // 2
    capacity = 16 * tok_count // experts_here
    per_group = TOPK // GLIM
    slots = tok_count // 2
    f32 = jnp.float32

    list_slot = expert_pick // experts_here
    member = expert_pick % experts_here
    pick_group = jnp.take_along_axis(group_list, list_slot, axis=1)
    group_ids = jnp.arange(group_count, dtype=jnp.int32)
    hit_group = (pick_group[:, :, None] == group_ids[None, None, :]).astype(jnp.int32)
    order = jnp.cumsum(hit_group, axis=1) - 1
    ordinal = jnp.sum(order * hit_group, axis=2)
    ord_ids = jnp.arange(per_group, dtype=jnp.int32)
    hit_ord = (ordinal[:, :, None] == ord_ids[None, None, :]).astype(jnp.int32)
    sel_tki = hit_group[:, :, :, None] * hit_ord[:, :, None, :]
    member_list = jnp.sum(sel_tki * member[:, :, None, None], axis=1)
    weight_list = jnp.sum(sel_tki.astype(f32) * route_weight.astype(f32)[:, :, None, None], axis=1)
    listed = jnp.sum((group_list[:, :, None] == group_ids[None, None, :]).astype(jnp.int32), axis=1)
    running = jnp.cumsum(listed, axis=0) - 1
    slot_ids = jnp.arange(slots, dtype=jnp.int32)
    placed = (listed.T[:, None, :] > 0) & (running.T[:, None, :] == slot_ids[None, :, None])
    placed_rows = placed.astype(jnp.bfloat16)
    placed_f = placed.astype(f32)
    token_meta = jnp.concatenate(
        [
            (member_list + 1).astype(f32).reshape(tok_count, group_count * per_group),
            weight_list.reshape(tok_count, group_count * per_group),
            jnp.zeros((tok_count, 128 - 2 * group_count * per_group), f32),
        ],
        axis=1,
    ).astype(jnp.bfloat16)
    token_all = jnp.concatenate([tokens, out_grad, token_meta], axis=1)
    packed = jnp.einsum(
        "gjt,tc->gjc", placed_rows, token_all, preferred_element_type=f32
    ).astype(jnp.bfloat16)
    arrived_all = lax.all_to_all(packed, "group", split_axis=0, concat_axis=0, tiled=True)
    me_group = lax.axis_index("group")
    meta_all = arrived_all[:, :, 2 * width :].astype(f32)
    own = (jnp.arange(128, dtype=jnp.int32) // per_group) == me_group
    own = own & (jnp.arange(128) < group_count * per_group)
    own_w = (
        ((jnp.arange(128, dtype=jnp.int32) - group_count * per_group) // per_group) == me_group
    ) & (jnp.arange(128) >= group_count * per_group) & (
        jnp.arange(128) < 2 * group_count * per_group
    )
    pos = jnp.arange(128, dtype=jnp.int32) % per_group
    pick_pos = (pos[:, None] == jnp.arange(per_group, dtype=jnp.int32)[None, :]).astype(f32)
    meta_members = jnp.einsum(
        "gjc,ci->gji", meta_all, own.astype(f32)[:, None] * pick_pos,
        precision=lax.Precision.HIGHEST,
    ) - 1.0
    meta_weights = jnp.einsum(
        "gjc,ci->gji", meta_all, own_w.astype(f32)[:, None] * pick_pos,
        precision=lax.Precision.HIGHEST,
    )
    arrived_meta = jnp.concatenate([meta_members, meta_weights], axis=2)

    arr_x = arrived_all[:, :, :width].reshape(-1, width)
    arr_dy = arrived_all[:, :, width : 2 * width].reshape(-1, width)
    flat_meta = arrived_meta.reshape(-1, 2 * per_group)
    arr_members = jnp.round(flat_meta[:, :per_group]).astype(jnp.int32)
    arr_weights = flat_meta[:, per_group:]
    member_ids = jnp.arange(experts_here, dtype=jnp.int32)
    matching = (arr_members[:, :, None] == member_ids[None, None, :]).astype(jnp.int32)
    flags = jnp.sum(matching, axis=1)
    rank = jnp.cumsum(flags, axis=0) - 1
    kept = (flags > 0) & (rank < capacity)
    cap_ids = jnp.arange(capacity, dtype=jnp.int32)
    sel = kept.T[:, None, :] & (rank.T[:, None, :] == cap_ids[None, :, None])
    sel_b = sel.astype(jnp.bfloat16)
    chooser = sel_b[:, :, :, None] * jnp.transpose(matching, (2, 0, 1))[:, None, :, :].astype(
        jnp.bfloat16
    )
    w_member = jnp.sum(matching.astype(f32) * arr_weights[:, :, None], axis=1)
    w_slot = jnp.einsum("msr,rm->ms", sel.astype(f32), w_member, precision=lax.Precision.HIGHEST)
    sel_2 = jnp.repeat(sel_b, 2, axis=0)
    w_slot_2 = jnp.repeat(w_slot, 2, axis=0)
    buf_x = jnp.einsum("msr,rd->msd", sel_2, arr_x, preferred_element_type=f32).astype(
        jnp.bfloat16
    )
    buf_dy = jnp.einsum("msr,rd->msd", sel_2, arr_dy, preferred_element_type=f32)
    buf_scaled = (w_slot_2[:, :, None] * buf_dy).astype(jnp.bfloat16)

    w_gate = gate_weight[0]
    w_up = up_weight[0]
    w_down = down_weight[0]
    inputs_here = to_owners(buf_x)
    gate, lifted, hidden, partial_value = expert_forward(inputs_here, w_gate, w_up, w_down)
    grads_here = to_owners(buf_scaled)
    partial_value, grads_here = lax.optimization_barrier(
        (partial_value.astype(jnp.bfloat16), grads_here)
    )
    outputs = lax.all_to_all(
        partial_value.reshape(2 * experts_here, capacity, width), "local", split_axis=0,
        concat_axis=0, tiled=True,
    )
    grad_gate, grad_up, grad_down, input_part = expert_backward(
        inputs_here, grads_here, gate, lifted, hidden, w_gate, w_up, w_down
    )
    input_part, grad_gate, grad_up, grad_down, outputs = lax.optimization_barrier(
        (input_part.astype(jnp.bfloat16), grad_gate, grad_up, grad_down, outputs)
    )
    input_grads = lax.all_to_all(
        input_part.reshape(2 * experts_here, capacity, width), "local", split_axis=0,
        concat_axis=0, tiled=True,
    )

    chooser_2 = jnp.repeat(chooser, 2, axis=0)
    out_pair = jnp.einsum("msri,msd->rid", chooser_2, outputs, preferred_element_type=f32)
    group_sum = jnp.sum(arr_weights[:, :, None] * out_pair, axis=1).astype(jnp.bfloat16)
    chooser_any = jnp.sum(chooser_2, axis=3)
    group_grad = jnp.einsum(
        "msr,msd->rd", chooser_any, input_grads, preferred_element_type=f32
    ).astype(jnp.bfloat16)
    pair_dw = jnp.sum(arr_dy.astype(f32)[:, None, :] * out_pair, axis=2).astype(jnp.bfloat16)
    back = jnp.concatenate(
        [
            group_sum.reshape(group_count, slots, width),
            jnp.zeros((group_count, slots, width), jnp.bfloat16),
            pair_dw.reshape(group_count, slots, per_group),
            jnp.zeros((group_count, slots, 128 - per_group), jnp.bfloat16),
        ],
        axis=2,
    )
    back = lax.dynamic_update_slice(
        back, group_grad.reshape(group_count, slots, width), (0, 0, width)
    )
    back_all = lax.all_to_all(back, "group", split_axis=0, concat_axis=0, tiled=True)
    dw_back = back_all[:, :, 2 * width : 2 * width + per_group]

    mixed = jnp.einsum(
        "gjt,gjd->td", placed_rows, back_all[:, :, :width], preferred_element_type=f32
    ).astype(jnp.bfloat16)
    token_grad = jnp.einsum(
        "gjt,gjd->td", placed_rows, back_all[:, :, width : 2 * width], preferred_element_type=f32
    ).astype(jnp.bfloat16)
    dw_token = jnp.einsum(
        "gjt,gji->tgi", placed_f, dw_back.astype(f32), precision=lax.Precision.HIGHEST
    )
    weight_grad = jnp.sum(sel_tki.astype(f32) * dw_token[:, None, :, :], axis=(2, 3)).astype(
        jnp.bfloat16
    )
    return (mixed, token_grad, weight_grad, grad_gate[None], grad_up[None], grad_down[None])


def solution(mesh):
    return jax.shard_map(
        local,
        mesh=mesh,
        in_specs=(
            P(("group", "local"), None),
            P(("group", "local"), None, None),
            P(("group", "local"), None, None),
            P(("group", "local"), None, None),
            P(("group", "local"), None),
            P(("group", "local"), None),
            P(("group", "local"), None),
            P(("group", "local"), None),
        ),
        out_specs=(
            P(("group", "local"), None),
            P(("group", "local"), None),
            P(("group", "local"), None),
            P(("group", "local"), None, None),
            P(("group", "local"), None, None),
            P(("group", "local"), None, None),
        ),
        check_vma=False,
    )
```

```python
import jax
import jax.numpy as jnp
from jax import lax
from jax.sharding import PartitionSpec as P

TOPK = 8
GLIM = 4


def to_owners(doubled):
    width = doubled.shape[-1]
    arrived = lax.all_to_all(doubled, "local", split_axis=0, concat_axis=0, tiled=True)
    return arrived.reshape(-1, width)


def expert_forward(inputs, w_gate, w_up, w_down):
    gate = jnp.dot(inputs, w_gate, preferred_element_type=jnp.float32)
    lifted = jnp.dot(inputs, w_up, preferred_element_type=jnp.float32)
    hidden = (gate * jax.nn.sigmoid(gate) * lifted).astype(jnp.bfloat16)
    partial_value = jnp.dot(hidden, w_down, preferred_element_type=jnp.float32)
    return (gate, lifted, hidden, partial_value)


def expert_backward(inputs, scaled, gate, lifted, hidden, w_gate, w_up, w_down):
    contract_last = (((1,), (1,)), ((), ()))
    contract_first = (((0,), (0,)), ((), ()))
    dhidden = lax.dot_general(scaled, w_down, contract_last, preferred_element_type=jnp.float32)
    grad_down = lax.dot_general(
        hidden, scaled, contract_first, preferred_element_type=jnp.float32
    ).astype(jnp.bfloat16)
    sig = jax.nn.sigmoid(gate)
    dgate = (dhidden * lifted * sig * (1.0 + gate * (1.0 - sig))).astype(jnp.bfloat16)
    dlift = (dhidden * gate * sig).astype(jnp.bfloat16)
    grad_gate = lax.dot_general(
        inputs, dgate, contract_first, preferred_element_type=jnp.float32
    ).astype(jnp.bfloat16)
    grad_up = lax.dot_general(
        inputs, dlift, contract_first, preferred_element_type=jnp.float32
    ).astype(jnp.bfloat16)
    input_part = lax.dot_general(
        dgate, w_gate, contract_last, preferred_element_type=jnp.float32
    ) + lax.dot_general(dlift, w_up, contract_last, preferred_element_type=jnp.float32)
    return (grad_gate, grad_up, grad_down, input_part)


def local(
    tokens, gate_weight, up_weight, down_weight, out_grad, group_list, expert_pick, route_weight
):
    tok_count, width = tokens.shape
    group_count = lax.axis_size("group")
    experts_here = lax.axis_size("local") // 2
    capacity = 16 * tok_count // experts_here
    per_group = TOPK // GLIM
    slots = tok_count // 2
    f32 = jnp.float32

    list_slot = expert_pick // experts_here
    member = expert_pick % experts_here
    pick_group = jnp.take_along_axis(group_list, list_slot, axis=1)
    group_ids = jnp.arange(group_count, dtype=jnp.int32)
    hit_group = (pick_group[:, :, None] == group_ids[None, None, :]).astype(jnp.int32)
    order = jnp.cumsum(hit_group, axis=1) - 1
    ordinal = jnp.sum(order * hit_group, axis=2)
    ord_ids = jnp.arange(per_group, dtype=jnp.int32)
    hit_ord = (ordinal[:, :, None] == ord_ids[None, None, :]).astype(jnp.int32)
    sel_tki = hit_group[:, :, :, None] * hit_ord[:, :, None, :]
    member_list = jnp.sum(sel_tki * member[:, :, None, None], axis=1)
    weight_list = jnp.sum(sel_tki.astype(f32) * route_weight.astype(f32)[:, :, None, None], axis=1)
    listed = jnp.sum((group_list[:, :, None] == group_ids[None, None, :]).astype(jnp.int32), axis=1)
    running = jnp.cumsum(listed, axis=0) - 1
    slot_ids = jnp.arange(slots, dtype=jnp.int32)
    placed = (listed.T[:, None, :] > 0) & (running.T[:, None, :] == slot_ids[None, :, None])
    placed_rows = placed.astype(jnp.bfloat16)
    placed_f = placed.astype(f32)
    token_meta = jnp.concatenate(
        [
            (member_list + 1).astype(f32).reshape(tok_count, group_count * per_group),
            weight_list.reshape(tok_count, group_count * per_group),
            jnp.zeros((tok_count, 128 - 2 * group_count * per_group), f32),
        ],
        axis=1,
    ).astype(jnp.bfloat16)
    token_all = jnp.concatenate([tokens, out_grad, token_meta], axis=1)
    packed = jnp.einsum(
        "gjt,tc->gjc", placed_rows, token_all, preferred_element_type=f32
    ).astype(jnp.bfloat16)
    arrived_all = lax.all_to_all(packed, "group", split_axis=0, concat_axis=0, tiled=True)
    me_group = lax.axis_index("group")
    meta_all = arrived_all[:, :, 2 * width :].astype(f32)
    own = (jnp.arange(128, dtype=jnp.int32) // per_group) == me_group
    own = own & (jnp.arange(128) < group_count * per_group)
    own_w = (
        ((jnp.arange(128, dtype=jnp.int32) - group_count * per_group) // per_group) == me_group
    ) & (jnp.arange(128) >= group_count * per_group) & (
        jnp.arange(128) < 2 * group_count * per_group
    )
    pos = jnp.arange(128, dtype=jnp.int32) % per_group
    pick_pos = (pos[:, None] == jnp.arange(per_group, dtype=jnp.int32)[None, :]).astype(f32)
    meta_members = jnp.einsum(
        "gjc,ci->gji", meta_all, own.astype(f32)[:, None] * pick_pos,
        precision=lax.Precision.HIGHEST,
    ) - 1.0
    meta_weights = jnp.einsum(
        "gjc,ci->gji", meta_all, own_w.astype(f32)[:, None] * pick_pos,
        precision=lax.Precision.HIGHEST,
    )
    arrived_meta = jnp.concatenate([meta_members, meta_weights], axis=2)

    arr_x = arrived_all[:, :, :width].reshape(-1, width)
    arr_dy = arrived_all[:, :, width : 2 * width].reshape(-1, width)
    flat_meta = arrived_meta.reshape(-1, 2 * per_group)
    arr_members = jnp.round(flat_meta[:, :per_group]).astype(jnp.int32)
    arr_weights = flat_meta[:, per_group:]
    member_ids = jnp.arange(experts_here, dtype=jnp.int32)
    matching = (arr_members[:, :, None] == member_ids[None, None, :]).astype(jnp.int32)
    flags = jnp.sum(matching, axis=1)
    rank = jnp.cumsum(flags, axis=0) - 1
    kept = (flags > 0) & (rank < capacity)
    cap_ids = jnp.arange(capacity, dtype=jnp.int32)
    sel = kept.T[:, None, :] & (rank.T[:, None, :] == cap_ids[None, :, None])
    sel_b = sel.astype(jnp.bfloat16)
    chooser = sel_b[:, :, :, None] * jnp.transpose(matching, (2, 0, 1))[:, None, :, :].astype(
        jnp.bfloat16
    )
    w_member = jnp.sum(matching.astype(f32) * arr_weights[:, :, None], axis=1)
    w_slot = jnp.einsum("msr,rm->ms", sel.astype(f32), w_member, precision=lax.Precision.HIGHEST)
    sel_2 = jnp.repeat(sel_b, 2, axis=0)
    w_slot_2 = jnp.repeat(w_slot, 2, axis=0)
    arrivals = arr_x.shape[0]
    row_ids = jnp.arange(arrivals, dtype=jnp.int32)
    slot_row = jnp.sum(sel.astype(jnp.int32) * row_ids[None, None, :], axis=2) + arrivals * (
        1 - jnp.sum(sel.astype(jnp.int32), axis=2)
    )
    x_rows = jnp.concatenate([arr_x, jnp.zeros((1, width), arr_x.dtype)], axis=0)
    buf_x = jnp.take(x_rows, jnp.repeat(slot_row, 2, axis=0).reshape(-1), axis=0).reshape(
        2 * experts_here, capacity, width
    )
    buf_dy = jnp.einsum("msr,rd->msd", sel_2, arr_dy, preferred_element_type=f32)
    buf_scaled = (w_slot_2[:, :, None] * buf_dy).astype(jnp.bfloat16)

    w_gate = gate_weight[0]
    w_up = up_weight[0]
    w_down = down_weight[0]
    inputs_here = to_owners(buf_x)
    gate, lifted, hidden, partial_value = expert_forward(inputs_here, w_gate, w_up, w_down)
    grads_here = to_owners(buf_scaled)
    partial_value, grads_here = lax.optimization_barrier(
        (partial_value.astype(jnp.bfloat16), grads_here)
    )
    outputs = lax.all_to_all(
        partial_value.reshape(2 * experts_here, capacity, width), "local", split_axis=0,
        concat_axis=0, tiled=True,
    )
    grad_gate, grad_up, grad_down, input_part = expert_backward(
        inputs_here, grads_here, gate, lifted, hidden, w_gate, w_up, w_down
    )
    input_part, grad_gate, grad_up, grad_down, outputs = lax.optimization_barrier(
        (input_part.astype(jnp.bfloat16), grad_gate, grad_up, grad_down, outputs)
    )
    input_grads = lax.all_to_all(
        input_part.reshape(2 * experts_here, capacity, width), "local", split_axis=0,
        concat_axis=0, tiled=True,
    )

    chooser_2 = jnp.repeat(chooser, 2, axis=0)
    out_pair = jnp.einsum("msri,msd->rid", chooser_2, outputs, preferred_element_type=f32)
    group_sum = jnp.sum(arr_weights[:, :, None] * out_pair, axis=1).astype(jnp.bfloat16)
    chooser_any = jnp.sum(chooser_2, axis=3)
    group_grad = jnp.einsum(
        "msr,msd->rd", chooser_any, input_grads, preferred_element_type=f32
    ).astype(jnp.bfloat16)
    pair_dw = jnp.sum(arr_dy.astype(f32)[:, None, :] * out_pair, axis=2).astype(jnp.bfloat16)
    back = jnp.concatenate(
        [
            group_sum.reshape(group_count, slots, width),
            jnp.zeros((group_count, slots, width), jnp.bfloat16),
            pair_dw.reshape(group_count, slots, per_group),
            jnp.zeros((group_count, slots, 128 - per_group), jnp.bfloat16),
        ],
        axis=2,
    )
    back = lax.dynamic_update_slice(
        back, group_grad.reshape(group_count, slots, width), (0, 0, width)
    )
    back_all = lax.all_to_all(back, "group", split_axis=0, concat_axis=0, tiled=True)
    dw_back = back_all[:, :, 2 * width : 2 * width + per_group]

    mixed = jnp.einsum(
        "gjt,gjd->td", placed_rows, back_all[:, :, :width], preferred_element_type=f32
    ).astype(jnp.bfloat16)
    token_grad = jnp.einsum(
        "gjt,gjd->td", placed_rows, back_all[:, :, width : 2 * width], preferred_element_type=f32
    ).astype(jnp.bfloat16)
    dw_token = jnp.einsum(
        "gjt,gji->tgi", placed_f, dw_back.astype(f32), precision=lax.Precision.HIGHEST
    )
    weight_grad = jnp.sum(sel_tki.astype(f32) * dw_token[:, None, :, :], axis=(2, 3)).astype(
        jnp.bfloat16
    )
    return (mixed, token_grad, weight_grad, grad_gate[None], grad_up[None], grad_down[None])


def solution(mesh):
    return jax.shard_map(
        local,
        mesh=mesh,
        in_specs=(
            P(("group", "local"), None),
            P(("group", "local"), None, None),
            P(("group", "local"), None, None),
            P(("group", "local"), None, None),
            P(("group", "local"), None),
            P(("group", "local"), None),
            P(("group", "local"), None),
            P(("group", "local"), None),
        ),
        out_specs=(
            P(("group", "local"), None),
            P(("group", "local"), None),
            P(("group", "local"), None),
            P(("group", "local"), None, None),
            P(("group", "local"), None, None),
            P(("group", "local"), None, None),
        ),
        check_vma=False,
    )
```

```python
import jax
import jax.numpy as jnp
from jax import lax
from jax.sharding import PartitionSpec as P

TOPK = 8
GLIM = 4


def to_owners(doubled):
    width = doubled.shape[-1]
    arrived = lax.all_to_all(doubled, "local", split_axis=0, concat_axis=0, tiled=True)
    return arrived.reshape(-1, width)


def expert_forward(inputs, w_gate, w_up, w_down):
    gate = jnp.dot(inputs, w_gate, preferred_element_type=jnp.float32)
    lifted = jnp.dot(inputs, w_up, preferred_element_type=jnp.float32)
    hidden = (gate * jax.nn.sigmoid(gate) * lifted).astype(jnp.bfloat16)
    partial_value = jnp.dot(hidden, w_down, preferred_element_type=jnp.float32)
    return (gate, lifted, hidden, partial_value)


def expert_backward(inputs, scaled, gate, lifted, hidden, w_gate, w_up, w_down):
    contract_last = (((1,), (1,)), ((), ()))
    contract_first = (((0,), (0,)), ((), ()))
    dhidden = lax.dot_general(scaled, w_down, contract_last, preferred_element_type=jnp.float32)
    grad_down = lax.dot_general(
        hidden, scaled, contract_first, preferred_element_type=jnp.float32
    ).astype(jnp.bfloat16)
    sig = jax.nn.sigmoid(gate)
    dgate = (dhidden * lifted * sig * (1.0 + gate * (1.0 - sig))).astype(jnp.bfloat16)
    dlift = (dhidden * gate * sig).astype(jnp.bfloat16)
    grad_gate = lax.dot_general(
        inputs, dgate, contract_first, preferred_element_type=jnp.float32
    ).astype(jnp.bfloat16)
    grad_up = lax.dot_general(
        inputs, dlift, contract_first, preferred_element_type=jnp.float32
    ).astype(jnp.bfloat16)
    input_part = lax.dot_general(
        dgate, w_gate, contract_last, preferred_element_type=jnp.float32
    ) + lax.dot_general(dlift, w_up, contract_last, preferred_element_type=jnp.float32)
    return (grad_gate, grad_up, grad_down, input_part)


def local(
    tokens, gate_weight, up_weight, down_weight, out_grad, group_list, expert_pick, route_weight
):
    tok_count, width = tokens.shape
    group_count = lax.axis_size("group")
    experts_here = lax.axis_size("local") // 2
    capacity = 16 * tok_count // experts_here
    per_group = TOPK // GLIM
    slots = tok_count // 2
    f32 = jnp.float32

    list_slot = expert_pick // experts_here
    member = expert_pick % experts_here
    slot_hit = list_slot[:, :, None] == jnp.arange(GLIM, dtype=jnp.int32)[None, None, :]
    pick_group = jnp.sum(jnp.where(slot_hit, group_list[:, None, :], 0), axis=2)
    group_ids = jnp.arange(group_count, dtype=jnp.int32)
    hit_group = (pick_group[:, :, None] == group_ids[None, None, :]).astype(jnp.int32)
    order = jnp.cumsum(hit_group, axis=1) - 1
    ordinal = jnp.sum(order * hit_group, axis=2)
    ord_ids = jnp.arange(per_group, dtype=jnp.int32)
    hit_ord = (ordinal[:, :, None] == ord_ids[None, None, :]).astype(jnp.int32)
    sel_tki = hit_group[:, :, :, None] * hit_ord[:, :, None, :]
    member_list = jnp.sum(sel_tki * member[:, :, None, None], axis=1)
    weight_list = jnp.sum(sel_tki.astype(f32) * route_weight.astype(f32)[:, :, None, None], axis=1)
    listed = jnp.sum((group_list[:, :, None] == group_ids[None, None, :]).astype(jnp.int32), axis=1)
    running = jnp.cumsum(listed, axis=0) - 1
    slot_ids = jnp.arange(slots, dtype=jnp.int32)
    placed = (listed.T[:, None, :] > 0) & (running.T[:, None, :] == slot_ids[None, :, None])
    placed_rows = placed.astype(jnp.bfloat16)
    placed_f = placed.astype(f32)
    token_meta = jnp.concatenate(
        [
            (member_list + 1).astype(f32).reshape(tok_count, group_count * per_group),
            weight_list.reshape(tok_count, group_count * per_group),
            jnp.zeros((tok_count, 128 - 2 * group_count * per_group), f32),
        ],
        axis=1,
    ).astype(jnp.bfloat16)
    token_all = jnp.concatenate([tokens, out_grad, token_meta], axis=1)
    packed = jnp.einsum(
        "gjt,tc->gjc", placed_rows, token_all, preferred_element_type=f32
    ).astype(jnp.bfloat16)
    arrived_all = lax.all_to_all(packed, "group", split_axis=0, concat_axis=0, tiled=True)
    me_group = lax.axis_index("group")
    meta_all = arrived_all[:, :, 2 * width :].astype(f32)
    own = (jnp.arange(128, dtype=jnp.int32) // per_group) == me_group
    own = own & (jnp.arange(128) < group_count * per_group)
    own_w = (
        ((jnp.arange(128, dtype=jnp.int32) - group_count * per_group) // per_group) == me_group
    ) & (jnp.arange(128) >= group_count * per_group) & (
        jnp.arange(128) < 2 * group_count * per_group
    )
    pos = jnp.arange(128, dtype=jnp.int32) % per_group
    pick_pos = (pos[:, None] == jnp.arange(per_group, dtype=jnp.int32)[None, :]).astype(f32)
    meta_members = jnp.einsum(
        "gjc,ci->gji", meta_all, own.astype(f32)[:, None] * pick_pos,
        precision=lax.Precision.HIGHEST,
    ) - 1.0
    meta_weights = jnp.einsum(
        "gjc,ci->gji", meta_all, own_w.astype(f32)[:, None] * pick_pos,
        precision=lax.Precision.HIGHEST,
    )
    arrived_meta = jnp.concatenate([meta_members, meta_weights], axis=2)

    arr_x = arrived_all[:, :, :width].reshape(-1, width)
    arr_dy = arrived_all[:, :, width : 2 * width].reshape(-1, width)
    flat_meta = arrived_meta.reshape(-1, 2 * per_group)
    arr_members = jnp.round(flat_meta[:, :per_group]).astype(jnp.int32)
    arr_weights = flat_meta[:, per_group:]
    member_ids = jnp.arange(experts_here, dtype=jnp.int32)
    matching = (arr_members[:, :, None] == member_ids[None, None, :]).astype(jnp.int32)
    flags = jnp.sum(matching, axis=1)
    rank = jnp.cumsum(flags, axis=0) - 1
    kept = (flags > 0) & (rank < capacity)
    cap_ids = jnp.arange(capacity, dtype=jnp.int32)
    sel = kept.T[:, None, :] & (rank.T[:, None, :] == cap_ids[None, :, None])
    sel_b = sel.astype(jnp.bfloat16)
    chooser = sel_b[:, :, :, None] * jnp.transpose(matching, (2, 0, 1))[:, None, :, :].astype(
        jnp.bfloat16
    )
    w_member = jnp.sum(matching.astype(f32) * arr_weights[:, :, None], axis=1)
    w_slot = jnp.einsum("msr,rm->ms", sel.astype(f32), w_member, precision=lax.Precision.HIGHEST)
    sel_2 = jnp.repeat(sel_b, 2, axis=0)
    w_slot_2 = jnp.repeat(w_slot, 2, axis=0)
    buf_x = jnp.einsum("msr,rd->msd", sel_2, arr_x, preferred_element_type=f32).astype(
        jnp.bfloat16
    )
    buf_dy = jnp.einsum("msr,rd->msd", sel_2, arr_dy, preferred_element_type=f32)
    buf_scaled = (w_slot_2[:, :, None] * buf_dy).astype(jnp.bfloat16)

    w_gate = gate_weight[0]
    w_up = up_weight[0]
    w_down = down_weight[0]
    inputs_here = to_owners(buf_x)
    gate, lifted, hidden, partial_value = expert_forward(inputs_here, w_gate, w_up, w_down)
    grads_here = to_owners(buf_scaled)
    partial_value, grads_here = lax.optimization_barrier(
        (partial_value.astype(jnp.bfloat16), grads_here)
    )
    outputs = lax.all_to_all(
        partial_value.reshape(2 * experts_here, capacity, width), "local", split_axis=0,
        concat_axis=0, tiled=True,
    )
    grad_gate, grad_up, grad_down, input_part = expert_backward(
        inputs_here, grads_here, gate, lifted, hidden, w_gate, w_up, w_down
    )
    input_part, grad_gate, grad_up, grad_down, outputs = lax.optimization_barrier(
        (input_part.astype(jnp.bfloat16), grad_gate, grad_up, grad_down, outputs)
    )
    input_grads = lax.all_to_all(
        input_part.reshape(2 * experts_here, capacity, width), "local", split_axis=0,
        concat_axis=0, tiled=True,
    )

    chooser_2 = jnp.repeat(chooser, 2, axis=0)
    out_pair = jnp.einsum("msri,msd->rid", chooser_2, outputs, preferred_element_type=f32)
    group_sum = jnp.sum(arr_weights[:, :, None] * out_pair, axis=1).astype(jnp.bfloat16)
    chooser_any = jnp.sum(chooser_2, axis=3)
    group_grad = jnp.einsum(
        "msr,msd->rd", chooser_any, input_grads, preferred_element_type=f32
    ).astype(jnp.bfloat16)
    pair_dw = jnp.sum(arr_dy.astype(f32)[:, None, :] * out_pair, axis=2).astype(jnp.bfloat16)
    back = jnp.concatenate(
        [
            group_sum.reshape(group_count, slots, width),
            jnp.zeros((group_count, slots, width), jnp.bfloat16),
            pair_dw.reshape(group_count, slots, per_group),
            jnp.zeros((group_count, slots, 128 - per_group), jnp.bfloat16),
        ],
        axis=2,
    )
    back = lax.dynamic_update_slice(
        back, group_grad.reshape(group_count, slots, width), (0, 0, width)
    )
    back_all = lax.all_to_all(back, "group", split_axis=0, concat_axis=0, tiled=True)
    dw_back = back_all[:, :, 2 * width : 2 * width + per_group]

    mixed = jnp.einsum(
        "gjt,gjd->td", placed_rows, back_all[:, :, :width], preferred_element_type=f32
    ).astype(jnp.bfloat16)
    token_grad = jnp.einsum(
        "gjt,gjd->td", placed_rows, back_all[:, :, width : 2 * width], preferred_element_type=f32
    ).astype(jnp.bfloat16)
    dw_token = jnp.einsum(
        "gjt,gji->tgi", placed_f, dw_back.astype(f32), precision=lax.Precision.HIGHEST
    )
    weight_grad = jnp.sum(sel_tki.astype(f32) * dw_token[:, None, :, :], axis=(2, 3)).astype(
        jnp.bfloat16
    )
    return (mixed, token_grad, weight_grad, grad_gate[None], grad_up[None], grad_down[None])


def solution(mesh):
    return jax.shard_map(
        local,
        mesh=mesh,
        in_specs=(
            P(("group", "local"), None),
            P(("group", "local"), None, None),
            P(("group", "local"), None, None),
            P(("group", "local"), None, None),
            P(("group", "local"), None),
            P(("group", "local"), None),
            P(("group", "local"), None),
            P(("group", "local"), None),
        ),
        out_specs=(
            P(("group", "local"), None),
            P(("group", "local"), None),
            P(("group", "local"), None),
            P(("group", "local"), None, None),
            P(("group", "local"), None, None),
            P(("group", "local"), None, None),
        ),
        check_vma=False,
    )
```

```python
import jax
import jax.numpy as jnp
from jax import lax
from jax.sharding import PartitionSpec as P

TOPK = 8
GLIM = 4


def to_owners(doubled):
    width = doubled.shape[-1]
    arrived = lax.all_to_all(doubled, "local", split_axis=0, concat_axis=0, tiled=True)
    return arrived.reshape(-1, width)


def expert_forward(inputs, w_gate, w_up, w_down):
    gate = jnp.dot(inputs, w_gate, preferred_element_type=jnp.float32)
    lifted = jnp.dot(inputs, w_up, preferred_element_type=jnp.float32)
    hidden = (gate * jax.nn.sigmoid(gate) * lifted).astype(jnp.bfloat16)
    partial_value = jnp.dot(hidden, w_down, preferred_element_type=jnp.float32)
    return (gate, lifted, hidden, partial_value)


def expert_backward(inputs, scaled, gate, lifted, hidden, w_gate, w_up, w_down):
    contract_last = (((1,), (1,)), ((), ()))
    contract_first = (((0,), (0,)), ((), ()))
    dhidden = lax.dot_general(scaled, w_down, contract_last, preferred_element_type=jnp.float32)
    grad_down = lax.dot_general(
        hidden, scaled, contract_first, preferred_element_type=jnp.float32
    ).astype(jnp.bfloat16)
    sig = jax.nn.sigmoid(gate)
    dgate = (dhidden * lifted * sig * (1.0 + gate * (1.0 - sig))).astype(jnp.bfloat16)
    dlift = (dhidden * gate * sig).astype(jnp.bfloat16)
    grad_gate = lax.dot_general(
        inputs, dgate, contract_first, preferred_element_type=jnp.float32
    ).astype(jnp.bfloat16)
    grad_up = lax.dot_general(
        inputs, dlift, contract_first, preferred_element_type=jnp.float32
    ).astype(jnp.bfloat16)
    input_part = lax.dot_general(
        dgate, w_gate, contract_last, preferred_element_type=jnp.float32
    ) + lax.dot_general(dlift, w_up, contract_last, preferred_element_type=jnp.float32)
    return (grad_gate, grad_up, grad_down, input_part)


def local(
    tokens, gate_weight, up_weight, down_weight, out_grad, group_list, expert_pick, route_weight
):
    tok_count, width = tokens.shape
    group_count = lax.axis_size("group")
    experts_here = lax.axis_size("local") // 2
    capacity = 16 * tok_count // experts_here
    per_group = TOPK // GLIM
    slots = tok_count // 2
    f32 = jnp.float32

    list_slot = expert_pick // experts_here
    member = expert_pick % experts_here
    slot_hit = list_slot[:, :, None] == jnp.arange(GLIM, dtype=jnp.int32)[None, None, :]
    pick_group = jnp.sum(jnp.where(slot_hit, group_list[:, None, :], 0), axis=2)
    group_ids = jnp.arange(group_count, dtype=jnp.int32)
    hit_group = (pick_group[:, :, None] == group_ids[None, None, :]).astype(jnp.int32)
    order = jnp.cumsum(hit_group, axis=1) - 1
    ordinal = jnp.sum(order * hit_group, axis=2)
    ord_ids = jnp.arange(per_group, dtype=jnp.int32)
    hit_ord = (ordinal[:, :, None] == ord_ids[None, None, :]).astype(jnp.int32)
    sel_tki = hit_group[:, :, :, None] * hit_ord[:, :, None, :]
    member_list = jnp.sum(sel_tki * member[:, :, None, None], axis=1)
    weight_list = jnp.sum(sel_tki.astype(f32) * route_weight.astype(f32)[:, :, None, None], axis=1)
    listed = jnp.sum((group_list[:, :, None] == group_ids[None, None, :]).astype(jnp.int32), axis=1)
    running = jnp.cumsum(listed, axis=0) - 1
    slot_ids = jnp.arange(slots, dtype=jnp.int32)
    placed = (listed.T[:, None, :] > 0) & (running.T[:, None, :] == slot_ids[None, :, None])
    placed_rows = placed.astype(jnp.bfloat16)
    placed_f = placed.astype(f32)
    token_meta = jnp.concatenate(
        [
            (member_list + 1).astype(f32).reshape(tok_count, group_count * per_group),
            weight_list.reshape(tok_count, group_count * per_group),
            jnp.zeros((tok_count, 128 - 2 * group_count * per_group), f32),
        ],
        axis=1,
    ).astype(jnp.bfloat16)
    token_all = jnp.concatenate([tokens, out_grad, token_meta], axis=1)
    packed = jnp.einsum(
        "gjt,tc->gjc", placed_rows, token_all, preferred_element_type=f32
    ).astype(jnp.bfloat16)
    arrived_all = lax.all_to_all(packed, "group", split_axis=0, concat_axis=0, tiled=True)
    me_group = lax.axis_index("group")
    meta_all = arrived_all[:, :, 2 * width :].astype(f32)
    meta_members = (
        lax.dynamic_slice_in_dim(meta_all, me_group * per_group, per_group, axis=2) - 1.0
    )
    meta_weights = lax.dynamic_slice_in_dim(
        meta_all, group_count * per_group + me_group * per_group, per_group, axis=2
    )
    arrived_meta = jnp.concatenate([meta_members, meta_weights], axis=2)

    arr_x = arrived_all[:, :, :width].reshape(-1, width)
    arr_dy = arrived_all[:, :, width : 2 * width].reshape(-1, width)
    flat_meta = arrived_meta.reshape(-1, 2 * per_group)
    arr_members = jnp.round(flat_meta[:, :per_group]).astype(jnp.int32)
    arr_weights = flat_meta[:, per_group:]
    member_ids = jnp.arange(experts_here, dtype=jnp.int32)
    matching = (arr_members[:, :, None] == member_ids[None, None, :]).astype(jnp.int32)
    flags = jnp.sum(matching, axis=1)
    rank = jnp.cumsum(flags, axis=0) - 1
    kept = (flags > 0) & (rank < capacity)
    cap_ids = jnp.arange(capacity, dtype=jnp.int32)
    sel = kept.T[:, None, :] & (rank.T[:, None, :] == cap_ids[None, :, None])
    sel_b = sel.astype(jnp.bfloat16)
    chooser = sel_b[:, :, :, None] * jnp.transpose(matching, (2, 0, 1))[:, None, :, :].astype(
        jnp.bfloat16
    )
    w_member = jnp.sum(matching.astype(f32) * arr_weights[:, :, None], axis=1)
    w_slot = jnp.einsum("msr,rm->ms", sel.astype(f32), w_member, precision=lax.Precision.HIGHEST)
    sel_2 = jnp.repeat(sel_b, 2, axis=0)
    w_slot_2 = jnp.repeat(w_slot, 2, axis=0)
    buf_x = jnp.einsum("msr,rd->msd", sel_2, arr_x, preferred_element_type=f32).astype(
        jnp.bfloat16
    )
    buf_dy = jnp.einsum("msr,rd->msd", sel_2, arr_dy, preferred_element_type=f32)
    buf_scaled = (w_slot_2[:, :, None] * buf_dy).astype(jnp.bfloat16)

    w_gate = gate_weight[0]
    w_up = up_weight[0]
    w_down = down_weight[0]
    inputs_here = to_owners(buf_x)
    gate, lifted, hidden, partial_value = expert_forward(inputs_here, w_gate, w_up, w_down)
    grads_here = to_owners(buf_scaled)
    partial_value, grads_here = lax.optimization_barrier(
        (partial_value.astype(jnp.bfloat16), grads_here)
    )
    outputs = lax.all_to_all(
        partial_value.reshape(2 * experts_here, capacity, width), "local", split_axis=0,
        concat_axis=0, tiled=True,
    )
    grad_gate, grad_up, grad_down, input_part = expert_backward(
        inputs_here, grads_here, gate, lifted, hidden, w_gate, w_up, w_down
    )
    input_part, grad_gate, grad_up, grad_down, outputs = lax.optimization_barrier(
        (input_part.astype(jnp.bfloat16), grad_gate, grad_up, grad_down, outputs)
    )
    input_grads = lax.all_to_all(
        input_part.reshape(2 * experts_here, capacity, width), "local", split_axis=0,
        concat_axis=0, tiled=True,
    )

    chooser_2 = jnp.repeat(chooser, 2, axis=0)
    out_pair = jnp.einsum("msri,msd->rid", chooser_2, outputs, preferred_element_type=f32)
    group_sum = jnp.sum(arr_weights[:, :, None] * out_pair, axis=1).astype(jnp.bfloat16)
    chooser_any = jnp.sum(chooser_2, axis=3)
    group_grad = jnp.einsum(
        "msr,msd->rd", chooser_any, input_grads, preferred_element_type=f32
    ).astype(jnp.bfloat16)
    pair_dw = jnp.sum(arr_dy.astype(f32)[:, None, :] * out_pair, axis=2).astype(jnp.bfloat16)
    back = jnp.concatenate(
        [
            group_sum.reshape(group_count, slots, width),
            jnp.zeros((group_count, slots, width), jnp.bfloat16),
            pair_dw.reshape(group_count, slots, per_group),
            jnp.zeros((group_count, slots, 128 - per_group), jnp.bfloat16),
        ],
        axis=2,
    )
    back = lax.dynamic_update_slice(
        back, group_grad.reshape(group_count, slots, width), (0, 0, width)
    )
    back_all = lax.all_to_all(back, "group", split_axis=0, concat_axis=0, tiled=True)
    dw_back = back_all[:, :, 2 * width : 2 * width + per_group]

    mixed = jnp.einsum(
        "gjt,gjd->td", placed_rows, back_all[:, :, :width], preferred_element_type=f32
    ).astype(jnp.bfloat16)
    token_grad = jnp.einsum(
        "gjt,gjd->td", placed_rows, back_all[:, :, width : 2 * width], preferred_element_type=f32
    ).astype(jnp.bfloat16)
    dw_token = jnp.einsum(
        "gjt,gji->tgi", placed_f, dw_back.astype(f32), precision=lax.Precision.HIGHEST
    )
    weight_grad = jnp.sum(sel_tki.astype(f32) * dw_token[:, None, :, :], axis=(2, 3)).astype(
        jnp.bfloat16
    )
    return (mixed, token_grad, weight_grad, grad_gate[None], grad_up[None], grad_down[None])


def solution(mesh):
    return jax.shard_map(
        local,
        mesh=mesh,
        in_specs=(
            P(("group", "local"), None),
            P(("group", "local"), None, None),
            P(("group", "local"), None, None),
            P(("group", "local"), None, None),
            P(("group", "local"), None),
            P(("group", "local"), None),
            P(("group", "local"), None),
            P(("group", "local"), None),
        ),
        out_specs=(
            P(("group", "local"), None),
            P(("group", "local"), None),
            P(("group", "local"), None),
            P(("group", "local"), None, None),
            P(("group", "local"), None, None),
            P(("group", "local"), None, None),
        ),
        check_vma=False,
    )
```

```python
import jax
import jax.numpy as jnp
from jax import lax
from jax.sharding import PartitionSpec as P

TOPK = 8
GLIM = 4


def to_owners(doubled):
    width = doubled.shape[-1]
    arrived = lax.all_to_all(doubled, "local", split_axis=0, concat_axis=0, tiled=True)
    return arrived.reshape(-1, width)


def expert_forward(inputs, w_gate, w_up, w_down):
    gate = jnp.dot(inputs, w_gate, preferred_element_type=jnp.float32)
    lifted = jnp.dot(inputs, w_up, preferred_element_type=jnp.float32)
    hidden = (gate * jax.nn.sigmoid(gate) * lifted).astype(jnp.bfloat16)
    partial_value = jnp.dot(hidden, w_down, preferred_element_type=jnp.float32)
    return (gate, lifted, hidden, partial_value)


def expert_backward(inputs, scaled, gate, lifted, hidden, w_gate, w_up, w_down):
    contract_last = (((1,), (1,)), ((), ()))
    contract_first = (((0,), (0,)), ((), ()))
    dhidden = lax.dot_general(scaled, w_down, contract_last, preferred_element_type=jnp.float32)
    grad_down = lax.dot_general(
        hidden, scaled, contract_first, preferred_element_type=jnp.float32
    ).astype(jnp.bfloat16)
    sig = jax.nn.sigmoid(gate)
    dgate = (dhidden * lifted * sig * (1.0 + gate * (1.0 - sig))).astype(jnp.bfloat16)
    dlift = (dhidden * gate * sig).astype(jnp.bfloat16)
    grad_gate = lax.dot_general(
        inputs, dgate, contract_first, preferred_element_type=jnp.float32
    ).astype(jnp.bfloat16)
    grad_up = lax.dot_general(
        inputs, dlift, contract_first, preferred_element_type=jnp.float32
    ).astype(jnp.bfloat16)
    input_part = lax.dot_general(
        dgate, w_gate, contract_last, preferred_element_type=jnp.float32
    ) + lax.dot_general(dlift, w_up, contract_last, preferred_element_type=jnp.float32)
    return (grad_gate, grad_up, grad_down, input_part)


def local(
    tokens, gate_weight, up_weight, down_weight, out_grad, group_list, expert_pick, route_weight
):
    tok_count, width = tokens.shape
    group_count = lax.axis_size("group")
    experts_here = lax.axis_size("local") // 2
    capacity = 16 * tok_count // experts_here
    per_group = TOPK // GLIM
    slots = tok_count // 2
    f32 = jnp.float32

    list_slot = expert_pick // experts_here
    member = expert_pick % experts_here
    slot_hit = list_slot[:, :, None] == jnp.arange(GLIM, dtype=jnp.int32)[None, None, :]
    pick_group = jnp.sum(jnp.where(slot_hit, group_list[:, None, :], 0), axis=2)
    group_ids = jnp.arange(group_count, dtype=jnp.int32)
    hit_group = (pick_group[:, :, None] == group_ids[None, None, :]).astype(jnp.int32)
    order = jnp.cumsum(hit_group, axis=1) - 1
    ordinal = jnp.sum(order * hit_group, axis=2)
    ord_ids = jnp.arange(per_group, dtype=jnp.int32)
    hit_ord = (ordinal[:, :, None] == ord_ids[None, None, :]).astype(jnp.int32)
    sel_tki = hit_group[:, :, :, None] * hit_ord[:, :, None, :]
    member_list = jnp.sum(sel_tki * member[:, :, None, None], axis=1)
    weight_list = jnp.sum(sel_tki.astype(f32) * route_weight.astype(f32)[:, :, None, None], axis=1)
    listed = jnp.sum((group_list[:, :, None] == group_ids[None, None, :]).astype(jnp.int32), axis=1)
    running = jnp.cumsum(listed, axis=0) - 1
    slot_ids = jnp.arange(slots, dtype=jnp.int32)
    placed = (listed.T[:, None, :] > 0) & (running.T[:, None, :] == slot_ids[None, :, None])
    placed_rows = placed.astype(jnp.bfloat16)
    placed_f = placed.astype(f32)
    token_meta = jnp.concatenate(
        [
            (member_list + 1).astype(f32).reshape(tok_count, group_count * per_group),
            weight_list.reshape(tok_count, group_count * per_group),
            jnp.zeros((tok_count, 128 - 2 * group_count * per_group), f32),
        ],
        axis=1,
    ).astype(jnp.bfloat16)
    token_all = jnp.concatenate([tokens, out_grad, token_meta], axis=1)
    packed = jnp.einsum(
        "gjt,tc->gjc", placed_rows, token_all, preferred_element_type=f32
    ).astype(jnp.bfloat16)
    arrived_all = lax.all_to_all(packed, "group", split_axis=0, concat_axis=0, tiled=True)
    me_group = lax.axis_index("group")
    meta_all = arrived_all[:, :, 2 * width :].astype(f32)
    meta_members = (
        lax.dynamic_slice_in_dim(meta_all, me_group * per_group, per_group, axis=2) - 1.0
    )
    meta_weights = lax.dynamic_slice_in_dim(
        meta_all, group_count * per_group + me_group * per_group, per_group, axis=2
    )
    arrived_meta = jnp.concatenate([meta_members, meta_weights], axis=2)

    arr_x = arrived_all[:, :, :width].reshape(-1, width)
    arr_dy = arrived_all[:, :, width : 2 * width].reshape(-1, width)
    flat_meta = arrived_meta.reshape(-1, 2 * per_group)
    arr_members = jnp.round(flat_meta[:, :per_group]).astype(jnp.int32)
    arr_weights = flat_meta[:, per_group:]
    member_ids = jnp.arange(experts_here, dtype=jnp.int32)
    matching = (arr_members[:, :, None] == member_ids[None, None, :]).astype(jnp.int32)
    flags = jnp.sum(matching, axis=1)
    rank = jnp.cumsum(flags, axis=0) - 1
    kept = (flags > 0) & (rank < capacity)
    cap_ids = jnp.arange(capacity, dtype=jnp.int32)
    sel = kept.T[:, None, :] & (rank.T[:, None, :] == cap_ids[None, :, None])
    sel_b = sel.astype(jnp.bfloat16)
    chooser = sel_b[:, :, :, None] * jnp.transpose(matching, (2, 0, 1))[:, None, :, :].astype(
        jnp.bfloat16
    )
    w_member = jnp.sum(matching.astype(f32) * arr_weights[:, :, None], axis=1)
    w_slot = jnp.einsum("msr,rm->ms", sel.astype(f32), w_member, precision=lax.Precision.HIGHEST)
    sel_2 = jnp.repeat(sel_b, 2, axis=0)
    w_slot_2 = jnp.repeat(w_slot, 2, axis=0)
    buf_x = jnp.einsum("msr,rd->msd", sel_2, arr_x, preferred_element_type=f32).astype(
        jnp.bfloat16
    )
    buf_dy = jnp.einsum("msr,rd->msd", sel_2, arr_dy, preferred_element_type=f32)
    buf_scaled = (w_slot_2[:, :, None] * buf_dy).astype(jnp.bfloat16)

    w_gate = gate_weight[0]
    w_up = up_weight[0]
    w_down = down_weight[0]
    inputs_here = to_owners(buf_x)
    gate, lifted, hidden, partial_value = expert_forward(inputs_here, w_gate, w_up, w_down)
    grads_here = to_owners(buf_scaled)
    partial_value, grads_here = lax.optimization_barrier(
        (partial_value.astype(jnp.bfloat16), grads_here)
    )
    outputs = lax.all_to_all(
        partial_value.reshape(2 * experts_here, capacity, width), "local", split_axis=0,
        concat_axis=0, tiled=True,
    )
    grad_gate, grad_up, grad_down, input_part = expert_backward(
        inputs_here, grads_here, gate, lifted, hidden, w_gate, w_up, w_down
    )
    input_part, grad_gate, grad_up, grad_down, outputs = lax.optimization_barrier(
        (input_part.astype(jnp.bfloat16), grad_gate, grad_up, grad_down, outputs)
    )
    input_grads = lax.all_to_all(
        input_part.reshape(2 * experts_here, capacity, width), "local", split_axis=0,
        concat_axis=0, tiled=True,
    )

    chooser_2 = jnp.repeat(chooser, 2, axis=0)
    out_pair = jnp.einsum("msri,msd->rid", chooser_2, outputs, preferred_element_type=f32)
    group_sum = jnp.sum(arr_weights[:, :, None] * out_pair, axis=1).astype(jnp.bfloat16)
    chooser_any = jnp.sum(chooser_2, axis=3)
    group_grad = jnp.einsum(
        "msr,msd->rd", chooser_any, input_grads, preferred_element_type=f32
    ).astype(jnp.bfloat16)
    pair_dw = jnp.sum(arr_dy.astype(f32)[:, None, :] * out_pair, axis=2).astype(jnp.bfloat16)
    back = jnp.concatenate(
        [
            group_sum.reshape(group_count, slots, width),
            jnp.zeros((group_count, slots, width), jnp.bfloat16),
            pair_dw.reshape(group_count, slots, per_group),
            jnp.zeros((group_count, slots, 128 - per_group), jnp.bfloat16),
        ],
        axis=2,
    )
    back = lax.dynamic_update_slice(
        back, group_grad.reshape(group_count, slots, width), (0, 0, width)
    )
    back_all = lax.all_to_all(back, "group", split_axis=0, concat_axis=0, tiled=True)
    dw_back = back_all[:, :, 2 * width : 2 * width + per_group]

    per_token = jnp.einsum(
        "gjt,gjd->td", placed_rows, back_all[:, :, : 2 * width], preferred_element_type=f32
    ).astype(jnp.bfloat16)
    mixed = per_token[:, :width]
    token_grad = per_token[:, width:]
    dw_token = jnp.einsum(
        "gjt,gji->tgi", placed_f, dw_back.astype(f32), precision=lax.Precision.HIGHEST
    )
    weight_grad = jnp.sum(sel_tki.astype(f32) * dw_token[:, None, :, :], axis=(2, 3)).astype(
        jnp.bfloat16
    )
    return (mixed, token_grad, weight_grad, grad_gate[None], grad_up[None], grad_down[None])


def solution(mesh):
    return jax.shard_map(
        local,
        mesh=mesh,
        in_specs=(
            P(("group", "local"), None),
            P(("group", "local"), None, None),
            P(("group", "local"), None, None),
            P(("group", "local"), None, None),
            P(("group", "local"), None),
            P(("group", "local"), None),
            P(("group", "local"), None),
            P(("group", "local"), None),
        ),
        out_specs=(
            P(("group", "local"), None),
            P(("group", "local"), None),
            P(("group", "local"), None),
            P(("group", "local"), None, None),
            P(("group", "local"), None, None),
            P(("group", "local"), None, None),
        ),
        check_vma=False,
    )
```
